512 devices in a mesh: seq: 32 (over z, core), fsdp: 16 (over x, y).
Axes of the slice: x: 4, y: 4, z: 16, core: 2. Of those that a mesh axis runs over, the one named last changes fastest.
Arguments:
- tokens: bfloat16 [12288, 2048], P('seq'), may hold values from -6 to 6
- w_query: bfloat16 [2048, 2048], P('seq', 'fsdp'), may hold values from -0.125 to 0.125
- w_key: bfloat16 [2048, 2048], P('seq', 'fsdp'), may hold values from -0.125 to 0.125
- w_value: bfloat16 [2048, 2048], P('seq', 'fsdp'), may hold values from -0.125 to 0.125
- norm_gain: float32 [2048], P('fsdp'), may hold values from 0.1 to 1.9
- block_mask: int32 [32, 3, 3], P('seq'), may hold values 0 or 1
- cotangent: bfloat16 [12288, 2048], P('seq', 'fsdp'), may hold values from -6 to 6
Outputs:
- attended: bfloat16 [12288, 2048], P('seq', 'fsdp')
- grad_tokens: bfloat16 [12288, 2048], P('seq', 'fsdp')
- grad_query: bfloat16 [2048, 2048], P('seq', 'fsdp')
- grad_key: bfloat16 [2048, 2048], P('seq', 'fsdp')
- grad_value: bfloat16 [2048, 2048], P('seq', 'fsdp')
The draws below stay inside these ranges and needn't reach their ends.
All inputs are finite; a program needn't handle non-finite values. No bound on the sum of `block_mask` on one device may be relied on, other than what follows from the above.
Results may differ from the reference program's by a relative error of at most 0.035.
Values may be sent and summed in bfloat16 or wider, within the bound.
No kernel may reach another device: no remote copies, remote signals or barrier semaphores. Data moves between devices by JAX's collectives and lax.ppermute only.
A program may use at most 64 MiB of HBM per device.

```python
import math
import jax
import jax.numpy as jnp
from jax import lax

D = 2048
HDIM = 128
BLOCK = 128
SEG = 384
NB = 3
HEADS = 16
HD = 2048
TOKENS = 12288
N_SEQ = 32


def place_ends(entries, key, smallest, largest):
    spot = [jax.random.randint(jax.random.fold_in(key, axis), (), 0, length) for axis, length in enumerate(entries.shape)]
    widest = entries.shape.index(max(entries.shape))
    beside = spot[:widest] + [(spot[widest] + 1) % entries.shape[widest]] + spot[widest + 1:]
    return entries.at[tuple(spot)].set(smallest).at[tuple(beside)].set(largest)


def spiked(drawn, rng, source, target, parts, factor):
    def block_of(dim):
        return (jnp.arange(drawn.shape[dim]) // (drawn.shape[dim] // parts)).reshape((-1,) + (1,) * (drawn.ndim - 1 - dim))

    first = jax.random.permutation(rng, parts)[block_of(target)]
    other_side = (block_of(target) + parts // 2) % parts
    return jnp.where((block_of(source) == first) | (block_of(source) == other_side), factor * drawn, drawn)


def level_of(rng, dims, pieces, smallest, high):
    def one(axis_at, blocks):
        draws = jax.random.uniform(jax.random.fold_in(jax.random.fold_in(rng, 6), axis_at), (blocks,), jnp.float32, smallest / len(pieces), high / len(pieces))
        return jnp.repeat(jnp.exp(draws), dims[axis_at] // blocks).reshape((-1,) + (1,) * (len(dims) - axis_at - 1))

    factor_of = one(*pieces[0])
    for cut in pieces[1:]:
        factor_of = factor_of * one(*cut)
    return factor_of


def gaussian(key, dims, spread, most, cuts=(), kind=jnp.bfloat16):
    gain = level_of(key, dims, cuts, -0.22, 0.18) if cuts else 1.0
    array = jax.random.normal(key, dims, jnp.float32) * spread * gain
    return jnp.minimum(jnp.maximum(array, -most), most).astype(kind)


def gaussian_with(key, dims, spread, limit, shards, heavy, held_as=jnp.bfloat16):
    entries = spread * jax.random.normal(key, dims, jnp.float32)
    if shards:
        entries = entries * level_of(key, dims, shards, -0.22, 0.18)
    return jnp.clip(spiked(entries, jax.random.fold_in(key, 3), *heavy), -limit, limit).astype(held_as)


def setup_inputs(seed: int = 0) -> dict:
    splits = jax.random.split(jax.random.key(seed), 8)
    tokens = gaussian_with(splits[0], (TOKENS, D), 1.0, 6.0, ((0, 32),), (0, 1, 32, 2.75))
    w_query = gaussian(splits[1], (D, HD), D ** -0.5, 0.125, ((0, 32), (1, 16)))
    w_key = gaussian(splits[2], (D, HD), D ** -0.5, 0.125, ((0, 32), (1, 16)))
    w_value = gaussian(splits[3], (D, HD), D ** -0.5, 0.125, ((0, 32), (1, 16)))
    norm_gain = jnp.clip(1.0 + 0.18 * jax.random.normal(splits[4], (HD,), jnp.float32), 0.1, 1.9)
    block_mask = place_ends((jax.random.randint(splits[5], (N_SEQ, NB, NB), 0, 2) < 1).astype(jnp.int32), jax.random.fold_in(splits[5], 1), 0, 1)
    cotangent = gaussian(splits[6], (TOKENS, HD), 1.0, 6.0, ((0, 32), (1, 16)))
    return dict(tokens=tokens, w_query=w_query, w_key=w_key, w_value=w_value, norm_gain=norm_gain, block_mask=block_mask, cotangent=cotangent)


EPSILON = 1e-06
EXACT = lax.Precision.HIGHEST

def rounded(value):
    return lax.optimization_barrier(value.astype(jnp.bfloat16))

def widened(value):
    return value.astype(jnp.float32)

def allowed_pairs(pattern):
    positions = jnp.arange(SEG)
    block_ids = positions // BLOCK
    selector = (block_ids[:, None] == jnp.arange(NB)[None, :]).astype(jnp.float32)
    spread_out = jnp.dot(jnp.dot(selector, pattern.astype(jnp.float32), precision=EXACT), selector.T, precision=EXACT)
    same_block = (block_ids[:, None] == block_ids[None, :]) & (positions[None, :] <= positions[:, None])
    earlier_block = (block_ids[None, :] < block_ids[:, None]) & (spread_out > 0.5)
    return same_block | earlier_block

def reference(tokens, w_query, w_key, w_value, norm_gain, block_mask, cotangent):
    weight_cat = jnp.concatenate([w_query, w_key, w_value], axis=1)
    projected = rounded(jnp.dot(widened(tokens), widened(weight_cat), precision=EXACT))
    queries = projected[:, :HD].reshape(N_SEQ, SEG, HEADS, HDIM)
    key_heads = projected[:, HD:2 * HD].reshape(N_SEQ, SEG, HEADS, HDIM)
    value_heads = projected[:, 2 * HD:].reshape(N_SEQ, SEG, HEADS, HDIM)
    increment = jnp.einsum('cthd,cthe->chde', widened(key_heads), widened(value_heads), precision=EXACT)
    running = jnp.cumsum(increment, axis=0)
    state = jnp.concatenate([jnp.zeros_like(increment[:1]), running[:-1]], axis=0)
    gain_heads = norm_gain.reshape(HEADS, HDIM)
    cot_heads = cotangent.reshape(N_SEQ, SEG, HEADS, HDIM)

    def forward_shard(items):
        query_part, key_part, value_part, state_part, pattern, cot_part = items
        allowed = allowed_pairs(pattern)
        state_low = widened(rounded(state_part))
        scores = jnp.einsum('shd,thd->hst', widened(query_part), widened(key_part), precision=EXACT)
        weights = widened(rounded(jnp.where(allowed[None], scores, 0.0)))
        mixed = jnp.einsum('shd,hde->she', widened(query_part), state_low, precision=EXACT)
        mixed = mixed + jnp.einsum('hst,the->she', weights, widened(value_part), precision=EXACT)
        scale = lax.rsqrt(lax.optimization_barrier(jnp.mean(mixed * mixed, axis=-1, keepdims=True)) + EPSILON)
        normed = mixed * scale
        attended = rounded(normed * gain_heads)
        given = widened(cot_part) * gain_heads
        d_mixed = rounded(scale * (given - normed * lax.optimization_barrier(jnp.mean(given * normed, axis=-1, keepdims=True))))
        d_state = jnp.einsum('shd,she->hde', widened(query_part), widened(d_mixed), precision=EXACT)
        return (attended, d_mixed, d_state)
    attended, d_mixed, d_state = lax.map(forward_shard, (queries, key_heads, value_heads, state, block_mask, cot_heads))
    behind = jnp.cumsum(d_state[::-1], axis=0)[::-1]
    later = jnp.concatenate([behind[1:], jnp.zeros_like(d_state[:1])], axis=0)

    def backward_shard(items):
        query_part, key_part, value_part, state_part, later_part, pattern, dmix_part = items
        allowed = allowed_pairs(pattern)
        state_low = widened(rounded(state_part))
        later_low = widened(rounded(later_part))
        query_wide = widened(query_part)
        key_wide = widened(key_part)
        value_wide = widened(value_part)
        dmix_wide = widened(dmix_part)
        scores = jnp.einsum('shd,thd->hst', query_wide, key_wide, precision=EXACT)
        weights = widened(rounded(jnp.where(allowed[None], scores, 0.0)))
        d_scores = jnp.einsum('she,the->hst', dmix_wide, value_wide, precision=EXACT)
        d_weights = widened(rounded(jnp.where(allowed[None], d_scores, 0.0)))
        d_queries = jnp.einsum('she,hde->shd', dmix_wide, state_low, precision=EXACT)
        d_queries = d_queries + jnp.einsum('hst,thd->shd', d_weights, key_wide, precision=EXACT)
        d_keys = jnp.einsum('hst,shd->thd', d_weights, query_wide, precision=EXACT)
        d_keys = d_keys + jnp.einsum('the,hde->thd', value_wide, later_low, precision=EXACT)
        d_values = jnp.einsum('hst,she->the', weights, dmix_wide, precision=EXACT)
        d_values = d_values + jnp.einsum('thd,hde->the', key_wide, later_low, precision=EXACT)
        return (rounded(d_queries), rounded(d_keys), rounded(d_values))
    d_queries, d_keys, d_values = lax.map(backward_shard, (queries, key_heads, value_heads, state, later, block_mask, d_mixed))
    grad_flat = [part.reshape(TOKENS, HEADS, HDIM) for part in (d_queries, d_keys, d_values)]
    grad_by_head = jnp.concatenate([jnp.transpose(part, (1, 0, 2)) for part in grad_flat], axis=2)
    weight_by_head = jnp.concatenate([jnp.transpose(part.reshape(D, HEADS, HDIM), (1, 0, 2)) for part in (w_query, w_key, w_value)], axis=2)

    def add_head(total, items):
        grad_head, weight_head = items
        term = jnp.dot(widened(grad_head), widened(weight_head).T, precision=EXACT)
        return (total + widened(rounded(term)), None)
    input_total, unused = lax.scan(add_head, jnp.zeros((TOKENS, D), jnp.float32), (grad_by_head, weight_by_head))
    grad_tokens = input_total.astype(jnp.bfloat16)
    grad_cat = jnp.concatenate([part.reshape(TOKENS, HD) for part in grad_flat], axis=1).reshape(N_SEQ, SEG, 3 * HD)

    def add_shard(total, items):
        token_part, grad_part = items
        term = jnp.dot(widened(token_part).T, widened(grad_part), precision=EXACT)
        return (total + widened(rounded(term)), None)
    weight_total, unused_two = lax.scan(add_shard, jnp.zeros((D, 3 * HD), jnp.float32), (tokens.reshape(N_SEQ, SEG, D), grad_cat))
    weight_total = (weight_total * (1.0 / math.sqrt(TOKENS))).astype(jnp.bfloat16)
    return (attended.reshape(TOKENS, HD), grad_tokens, weight_total[:, :HD], weight_total[:, HD:2 * HD], weight_total[:, 2 * HD:])
```

```python
import math

import jax
import jax.numpy as jnp
from jax import lax
from jax.sharding import PartitionSpec as P

HDIM = 128
BLOCK = 128
SEG = 384
NB = 3


EPSILON = 1e-06


def entering(array, axis, backward):
    count = lax.axis_size(axis)
    place = lax.axis_index(axis)
    gathered = lax.all_gather(array.astype(jnp.bfloat16), axis)
    source = jnp.arange(count)
    chosen = source > place if backward else source < place
    flat = gathered.reshape(count, -1)
    total = jnp.dot(chosen.astype(jnp.bfloat16), flat, preferred_element_type=jnp.float32)
    return total.reshape(array.shape)


def allowed_pairs(pattern):
    positions = jnp.arange(SEG)
    block_ids = positions // BLOCK
    selector = (block_ids[:, None] == jnp.arange(NB)[None, :]).astype(jnp.float32)
    spread_out = jnp.dot(
        jnp.dot(selector, pattern.astype(jnp.float32), precision=lax.Precision.HIGHEST),
        selector.T,
        precision=lax.Precision.HIGHEST,
    )
    same_block = (block_ids[:, None] == block_ids[None, :]) & (
        positions[None, :] <= positions[:, None]
    )
    earlier_block = (block_ids[None, :] < block_ids[:, None]) & (spread_out > 0.5)
    return same_block | earlier_block


def add_states(first_term, second_term):
    return first_term + second_term


def shards(tokens, w_query, w_key, w_value, norm_gain, block_mask, cotangent):
    columns = w_query.shape[1]
    heads_here = columns // HDIM
    allowed = allowed_pairs(block_mask[0])
    weight_cat = lax.all_gather(
        jnp.concatenate([w_query, w_key, w_value], axis=1), "seq", axis=0, tiled=True
    )
    projected = jnp.dot(tokens, weight_cat, preferred_element_type=jnp.float32)
    projected = projected.astype(jnp.bfloat16)
    queries = projected[:, :columns].reshape(SEG, heads_here, HDIM)
    key_heads = projected[:, columns : 2 * columns].reshape(SEG, heads_here, HDIM)
    value_heads = projected[:, 2 * columns :].reshape(SEG, heads_here, HDIM)
    increment = jnp.einsum(
        "thd,the->hde", key_heads, value_heads, preferred_element_type=jnp.float32
    )
    state = entering(increment, "seq", False)
    state_low = state.astype(jnp.bfloat16)
    scores = jnp.einsum("shd,thd->hst", queries, key_heads, preferred_element_type=jnp.float32)
    weights = jnp.where(allowed[None], scores, 0.0).astype(jnp.bfloat16)
    mixed = jnp.einsum("shd,hde->she", queries, state_low, preferred_element_type=jnp.float32)
    mixed = mixed + jnp.einsum(
        "hst,the->she", weights, value_heads, preferred_element_type=jnp.float32
    )
    scale = lax.rsqrt(jnp.mean(mixed * mixed, axis=-1, keepdims=True) + EPSILON)
    normed = mixed * scale
    gain_heads = norm_gain.reshape(heads_here, HDIM)
    attended = (normed * gain_heads).reshape(SEG, columns).astype(jnp.bfloat16)
    given = cotangent.reshape(SEG, heads_here, HDIM).astype(jnp.float32) * gain_heads
    d_mixed = (scale * (given - normed * jnp.mean(given * normed, axis=-1, keepdims=True))).astype(
        jnp.bfloat16
    )
    d_state = jnp.einsum("shd,she->hde", queries, d_mixed, preferred_element_type=jnp.float32)
    later = entering(d_state, "seq", True)
    later_low = later.astype(jnp.bfloat16)
    d_scores = jnp.einsum("she,the->hst", d_mixed, value_heads, preferred_element_type=jnp.float32)
    d_weights = jnp.where(allowed[None], d_scores, 0.0).astype(jnp.bfloat16)
    d_queries = jnp.einsum("she,hde->shd", d_mixed, state_low, preferred_element_type=jnp.float32)
    d_queries = d_queries + jnp.einsum(
        "hst,thd->shd", d_weights, key_heads, preferred_element_type=jnp.float32
    )
    d_keys = jnp.einsum("hst,shd->thd", d_weights, queries, preferred_element_type=jnp.float32)
    d_keys = d_keys + jnp.einsum(
        "the,hde->thd", value_heads, later_low, preferred_element_type=jnp.float32
    )
    d_values = jnp.einsum("hst,she->the", weights, d_mixed, preferred_element_type=jnp.float32)
    d_values = d_values + jnp.einsum(
        "thd,hde->the", key_heads, later_low, preferred_element_type=jnp.float32
    )
    grad_cat = jnp.concatenate(
        [part.reshape(SEG, columns).astype(jnp.bfloat16) for part in (d_queries, d_keys, d_values)],
        axis=1,
    )
    input_rows = lax.psum_scatter(
        lax.dot_general(
            weight_cat, grad_cat, (((1,), (1,)), ((), ())), preferred_element_type=jnp.float32
        ).astype(jnp.bfloat16),
        "fsdp",
        scatter_dimension=0,
        tiled=True,
    ).astype(jnp.float32)
    grad_tokens = input_rows.T.astype(jnp.bfloat16)
    weight_rows = lax.psum_scatter(
        lax.dot_general(
            tokens, grad_cat, (((0,), (0,)), ((), ())), preferred_element_type=jnp.float32
        ).astype(jnp.bfloat16),
        "seq",
        scatter_dimension=0,
        tiled=True,
    ).astype(jnp.float32)
    weight_rows = (weight_rows * (1.0 / math.sqrt(SEG * lax.axis_size("seq")))).astype(jnp.bfloat16)
    return (
        attended,
        grad_tokens,
        weight_rows[:, :columns],
        weight_rows[:, columns : 2 * columns],
        weight_rows[:, 2 * columns :],
    )


def solution(mesh):
    placed = (
        P("seq", None),
        P("seq", "fsdp"),
        P("seq", "fsdp"),
        P("seq", "fsdp"),
        P("fsdp"),
        P("seq", None, None),
        P("seq", "fsdp"),
    )
    return jax.shard_map(
        shards,
        mesh=mesh,
        in_specs=placed,
        out_specs=(
            P("seq", "fsdp"),
            P("seq", "fsdp"),
            P("seq", "fsdp"),
            P("seq", "fsdp"),
            P("seq", "fsdp"),
        ),
        check_vma=False,
    )
```

```python
import math

import jax
import jax.numpy as jnp
from jax import lax
from jax.sharding import PartitionSpec as P

HDIM = 128
BLOCK = 128
SEG = 384
NB = 3


EPSILON = 1e-06


def entering(array, axis, backward):
    count = lax.axis_size(axis)
    total = array
    step = 1
    while step < count:
        if backward:
            pairs = [(i, i - step) for i in range(step, count)]
        else:
            pairs = [(i, i + step) for i in range(count - step)]
        total = total + lax.ppermute(total, axis, pairs)
        step *= 2
    return total - array


def halving_scatter(term, axis):
    count = lax.axis_size(axis)
    place = lax.axis_index(axis)
    rows = term.shape[0] // count
    current = term.astype(jnp.float32).reshape(count, rows, term.shape[1])
    bit = 0
    while (1 << bit) < count:
        mine = (place >> bit) & 1
        split = current.reshape(current.shape[0] // 2, 2, rows, term.shape[1])
        keep = lax.dynamic_index_in_dim(split, mine, 1, False)
        away = lax.dynamic_index_in_dim(split, 1 - mine, 1, False)
        pairs = [(i, i ^ (1 << bit)) for i in range(count)]
        current = keep + lax.ppermute(away.astype(jnp.bfloat16), axis, pairs).astype(jnp.float32)
        bit += 1
    return current.reshape(rows, term.shape[1])


def allowed_pairs(pattern):
    positions = jnp.arange(SEG)
    block_ids = positions // BLOCK
    selector = (block_ids[:, None] == jnp.arange(NB)[None, :]).astype(jnp.float32)
    spread_out = jnp.dot(
        jnp.dot(selector, pattern.astype(jnp.float32), precision=lax.Precision.HIGHEST),
        selector.T,
        precision=lax.Precision.HIGHEST,
    )
    same_block = (block_ids[:, None] == block_ids[None, :]) & (
        positions[None, :] <= positions[:, None]
    )
    earlier_block = (block_ids[None, :] < block_ids[:, None]) & (spread_out > 0.5)
    return same_block | earlier_block


def add_states(first_term, second_term):
    return first_term + second_term


def shards(tokens, w_query, w_key, w_value, norm_gain, block_mask, cotangent):
    columns = w_query.shape[1]
    heads_here = columns // HDIM
    allowed = allowed_pairs(block_mask[0])
    weight_cat = lax.all_gather(
        jnp.concatenate([w_query, w_key, w_value], axis=1), "seq", axis=0, tiled=True
    )
    projected = jnp.dot(tokens, weight_cat, preferred_element_type=jnp.float32)
    projected = projected.astype(jnp.bfloat16)
    queries = projected[:, :columns].reshape(SEG, heads_here, HDIM)
    key_heads = projected[:, columns : 2 * columns].reshape(SEG, heads_here, HDIM)
    value_heads = projected[:, 2 * columns :].reshape(SEG, heads_here, HDIM)
    increment = jnp.einsum(
        "thd,the->hde", key_heads, value_heads, preferred_element_type=jnp.float32
    )
    state = entering(increment, "seq", False)
    state_low = state.astype(jnp.bfloat16)
    scores = jnp.einsum("shd,thd->hst", queries, key_heads, preferred_element_type=jnp.float32)
    weights = jnp.where(allowed[None], scores, 0.0).astype(jnp.bfloat16)
    mixed = jnp.einsum("shd,hde->she", queries, state_low, preferred_element_type=jnp.float32)
    mixed = mixed + jnp.einsum(
        "hst,the->she", weights, value_heads, preferred_element_type=jnp.float32
    )
    scale = lax.rsqrt(jnp.mean(mixed * mixed, axis=-1, keepdims=True) + EPSILON)
    normed = mixed * scale
    gain_heads = norm_gain.reshape(heads_here, HDIM)
    attended = (normed * gain_heads).reshape(SEG, columns).astype(jnp.bfloat16)
    given = cotangent.reshape(SEG, heads_here, HDIM).astype(jnp.float32) * gain_heads
    d_mixed = (scale * (given - normed * jnp.mean(given * normed, axis=-1, keepdims=True))).astype(
        jnp.bfloat16
    )
    d_state = jnp.einsum("shd,she->hde", queries, d_mixed, preferred_element_type=jnp.float32)
    later = entering(d_state, "seq", True)
    later_low = later.astype(jnp.bfloat16)
    d_scores = jnp.einsum("she,the->hst", d_mixed, value_heads, preferred_element_type=jnp.float32)
    d_weights = jnp.where(allowed[None], d_scores, 0.0).astype(jnp.bfloat16)
    d_queries = jnp.einsum("she,hde->shd", d_mixed, state_low, preferred_element_type=jnp.float32)
    d_queries = d_queries + jnp.einsum(
        "hst,thd->shd", d_weights, key_heads, preferred_element_type=jnp.float32
    )
    d_keys = jnp.einsum("hst,shd->thd", d_weights, queries, preferred_element_type=jnp.float32)
    d_keys = d_keys + jnp.einsum(
        "the,hde->thd", value_heads, later_low, preferred_element_type=jnp.float32
    )
    d_values = jnp.einsum("hst,she->the", weights, d_mixed, preferred_element_type=jnp.float32)
    d_values = d_values + jnp.einsum(
        "thd,hde->the", key_heads, later_low, preferred_element_type=jnp.float32
    )
    grad_cat = jnp.concatenate(
        [part.reshape(SEG, columns).astype(jnp.bfloat16) for part in (d_queries, d_keys, d_values)],
        axis=1,
    )
    input_rows = lax.psum_scatter(
        lax.dot_general(
            weight_cat, grad_cat, (((1,), (1,)), ((), ())), preferred_element_type=jnp.float32
        ).astype(jnp.bfloat16),
        "fsdp",
        scatter_dimension=0,
        tiled=True,
    ).astype(jnp.float32)
    grad_tokens = input_rows.T.astype(jnp.bfloat16)
    weight_rows = halving_scatter(
        lax.dot_general(
            tokens, grad_cat, (((0,), (0,)), ((), ())), preferred_element_type=jnp.float32
        ).astype(jnp.bfloat16),
        "seq",
    )
    weight_rows = (weight_rows * (1.0 / math.sqrt(SEG * lax.axis_size("seq")))).astype(jnp.bfloat16)
    return (
        attended,
        grad_tokens,
        weight_rows[:, :columns],
        weight_rows[:, columns : 2 * columns],
        weight_rows[:, 2 * columns :],
    )


def solution(mesh):
    placed = (
        P("seq", None),
        P("seq", "fsdp"),
        P("seq", "fsdp"),
        P("seq", "fsdp"),
        P("fsdp"),
        P("seq", None, None),
        P("seq", "fsdp"),
    )
    return jax.shard_map(
        shards,
        mesh=mesh,
        in_specs=placed,
        out_specs=(
            P("seq", "fsdp"),
            P("seq", "fsdp"),
            P("seq", "fsdp"),
            P("seq", "fsdp"),
            P("seq", "fsdp"),
        ),
        check_vma=False,
    )
```

```python
import math

import jax
import jax.numpy as jnp
from jax import lax
from jax.sharding import Mesh, PartitionSpec as P

HDIM = 128
BLOCK = 128
SEG = 384
NB = 3


EPSILON = 1e-06
SEQ = ("z", "core")


def entering(array, axis, count, backward):
    total = array
    step = 1
    while step < count:
        parts = [total]
        for times in (1, 2, 3):
            shift = step * times
            if shift >= count:
                break
            if backward:
                pairs = [(i, i - shift) for i in range(shift, count)]
            else:
                pairs = [(i, i + shift) for i in range(count - shift)]
            parts.append(lax.ppermute(total, axis, pairs))
        total = sum(parts[1:], parts[0])
        step *= 4
    return total - array


def halving_scatter(term, axis, count):
    place = lax.axis_index(axis)
    rows = term.shape[0] // count
    current = term.astype(jnp.float32).reshape(count, rows, term.shape[1])
    bit = 0
    while (1 << bit) < count:
        mine = (place >> bit) & 1
        split = current.reshape(current.shape[0] // 2, 2, rows, term.shape[1])
        keep = lax.dynamic_index_in_dim(split, mine, 1, False)
        away = lax.dynamic_index_in_dim(split, 1 - mine, 1, False)
        pairs = [(i, i ^ (1 << bit)) for i in range(count)]
        current = keep + lax.ppermute(away.astype(jnp.bfloat16), axis, pairs).astype(jnp.float32)
        bit += 1
    return current.reshape(rows, term.shape[1])


def allowed_pairs(pattern):
    positions = jnp.arange(SEG)
    block_ids = positions // BLOCK
    selector = (block_ids[:, None] == jnp.arange(NB)[None, :]).astype(jnp.float32)
    spread_out = jnp.dot(
        jnp.dot(selector, pattern.astype(jnp.float32), precision=lax.Precision.HIGHEST),
        selector.T,
        precision=lax.Precision.HIGHEST,
    )
    same_block = (block_ids[:, None] == block_ids[None, :]) & (
        positions[None, :] <= positions[:, None]
    )
    earlier_block = (block_ids[None, :] < block_ids[:, None]) & (spread_out > 0.5)
    return same_block | earlier_block


def add_states(first_term, second_term):
    return first_term + second_term


def shards(tokens, w_query, w_key, w_value, norm_gain, block_mask, cotangent):
    columns = w_query.shape[1]
    heads_here = columns // HDIM
    allowed = allowed_pairs(block_mask[0])
    seq_count = lax.axis_size("z") * lax.axis_size("core")
    fsdp_count = lax.axis_size("fsdp")
    pair_rows = lax.all_gather(
        jnp.concatenate([w_query, w_key, w_value], axis=1), "core", axis=0, tiled=True
    )
    weight_cat = lax.all_gather(pair_rows, "z", axis=0, tiled=True)
    projected = jnp.dot(tokens, weight_cat, preferred_element_type=jnp.float32)
    projected = projected.astype(jnp.bfloat16)
    queries = projected[:, :columns].reshape(SEG, heads_here, HDIM)
    key_heads = projected[:, columns : 2 * columns].reshape(SEG, heads_here, HDIM)
    value_heads = projected[:, 2 * columns :].reshape(SEG, heads_here, HDIM)
    increment = jnp.einsum(
        "thd,the->hde", key_heads, value_heads, preferred_element_type=jnp.float32
    )
    state = entering(increment, SEQ, seq_count, False)
    state_low = state.astype(jnp.bfloat16)
    scores = jnp.einsum("shd,thd->hst", queries, key_heads, preferred_element_type=jnp.float32)
    weights = jnp.where(allowed[None], scores, 0.0).astype(jnp.bfloat16)
    mixed = jnp.einsum("shd,hde->she", queries, state_low, preferred_element_type=jnp.float32)
    mixed = mixed + jnp.einsum(
        "hst,the->she", weights, value_heads, preferred_element_type=jnp.float32
    )
    scale = lax.rsqrt(jnp.mean(mixed * mixed, axis=-1, keepdims=True) + EPSILON)
    normed = mixed * scale
    gain_heads = norm_gain.reshape(heads_here, HDIM)
    attended = (normed * gain_heads).reshape(SEG, columns).astype(jnp.bfloat16)
    given = cotangent.reshape(SEG, heads_here, HDIM).astype(jnp.float32) * gain_heads
    d_mixed = (scale * (given - normed * jnp.mean(given * normed, axis=-1, keepdims=True))).astype(
        jnp.bfloat16
    )
    d_state = jnp.einsum("shd,she->hde", queries, d_mixed, preferred_element_type=jnp.float32)
    later = entering(d_state, SEQ, seq_count, True)
    later_low = later.astype(jnp.bfloat16)
    d_scores = jnp.einsum("she,the->hst", d_mixed, value_heads, preferred_element_type=jnp.float32)
    d_weights = jnp.where(allowed[None], d_scores, 0.0).astype(jnp.bfloat16)
    d_queries = jnp.einsum("she,hde->shd", d_mixed, state_low, preferred_element_type=jnp.float32)
    d_queries = d_queries + jnp.einsum(
        "hst,thd->shd", d_weights, key_heads, preferred_element_type=jnp.float32
    )
    d_keys = jnp.einsum("hst,shd->thd", d_weights, queries, preferred_element_type=jnp.float32)
    d_keys = d_keys + jnp.einsum(
        "the,hde->thd", value_heads, later_low, preferred_element_type=jnp.float32
    )
    d_values = jnp.einsum("hst,she->the", weights, d_mixed, preferred_element_type=jnp.float32)
    d_values = d_values + jnp.einsum(
        "thd,hde->the", key_heads, later_low, preferred_element_type=jnp.float32
    )
    grad_cat = jnp.concatenate(
        [part.reshape(SEG, columns).astype(jnp.bfloat16) for part in (d_queries, d_keys, d_values)],
        axis=1,
    )
    input_rows = halving_scatter(
        lax.dot_general(
            weight_cat, grad_cat, (((1,), (1,)), ((), ())), preferred_element_type=jnp.float32
        ).astype(jnp.bfloat16),
        "fsdp",
        fsdp_count,
    )
    grad_tokens = input_rows.T.astype(jnp.bfloat16)
    weight_rows = halving_scatter(
        lax.dot_general(
            tokens, grad_cat, (((0,), (0,)), ((), ())), preferred_element_type=jnp.float32
        ).astype(jnp.bfloat16),
        SEQ,
        seq_count,
    )
    weight_rows = (weight_rows * (1.0 / math.sqrt(SEG * seq_count))).astype(jnp.bfloat16)
    return (
        attended,
        grad_tokens,
        weight_rows[:, :columns],
        weight_rows[:, columns : 2 * columns],
        weight_rows[:, 2 * columns :],
    )


def solution(mesh):
    split_mesh = Mesh(
        mesh.devices.reshape(mesh.shape["seq"] // 2, 2, mesh.shape["fsdp"]), ("z", "core", "fsdp")
    )
    placed = (
        P(SEQ, None),
        P(SEQ, "fsdp"),
        P(SEQ, "fsdp"),
        P(SEQ, "fsdp"),
        P("fsdp"),
        P(SEQ, None, None),
        P(SEQ, "fsdp"),
    )
    return jax.shard_map(
        shards,
        mesh=split_mesh,
        in_specs=placed,
        out_specs=(
            P(SEQ, "fsdp"),
            P(SEQ, "fsdp"),
            P(SEQ, "fsdp"),
            P(SEQ, "fsdp"),
            P(SEQ, "fsdp"),
        ),
        check_vma=False,
    )
```

```python
import math

import jax
import jax.numpy as jnp
from jax import lax
from jax.sharding import Mesh, PartitionSpec as P

HDIM = 128
BLOCK = 128
SEG = 384
NB = 3


EPSILON = 1e-06
SEQ = ("z", "core")


def entering(array, axis, count, backward):
    total = array
    step = 1
    while step < count:
        parts = [total]
        for times in (1, 2, 3):
            shift = step * times
            if shift >= count:
                break
            if backward:
                pairs = [(i, i - shift) for i in range(shift, count)]
            else:
                pairs = [(i, i + shift) for i in range(count - shift)]
            parts.append(lax.ppermute(total, axis, pairs))
        total = sum(parts[1:], parts[0])
        step *= 4
    return total - array


def gathered_by_exchange(array, axis, count):
    spread = jnp.broadcast_to(array[None], (count,) + array.shape)
    return lax.all_to_all(spread, axis, 0, 0)


def entering_exchange(array, axis, count, backward):
    place = lax.axis_index(axis)
    gathered = gathered_by_exchange(array.astype(jnp.bfloat16), axis, count)
    source = jnp.arange(count)
    chosen = source > place if backward else source < place
    flat = gathered.reshape(count, -1)
    total = jnp.dot(chosen.astype(jnp.bfloat16), flat, preferred_element_type=jnp.float32)
    return total.reshape(array.shape)


def halving_scatter(term, axis, count):
    place = lax.axis_index(axis)
    rows = term.shape[0] // count
    current = term.astype(jnp.float32).reshape(count, rows, term.shape[1])
    bit = 0
    while (1 << bit) < count:
        mine = (place >> bit) & 1
        split = current.reshape(current.shape[0] // 2, 2, rows, term.shape[1])
        keep = lax.dynamic_index_in_dim(split, mine, 1, False)
        away = lax.dynamic_index_in_dim(split, 1 - mine, 1, False)
        pairs = [(i, i ^ (1 << bit)) for i in range(count)]
        current = keep + lax.ppermute(away.astype(jnp.bfloat16), axis, pairs).astype(jnp.float32)
        bit += 1
    return current.reshape(rows, term.shape[1])


def allowed_pairs(pattern):
    positions = jnp.arange(SEG)
    block_ids = positions // BLOCK
    selector = (block_ids[:, None] == jnp.arange(NB)[None, :]).astype(jnp.float32)
    spread_out = jnp.dot(
        jnp.dot(selector, pattern.astype(jnp.float32), precision=lax.Precision.HIGHEST),
        selector.T,
        precision=lax.Precision.HIGHEST,
    )
    same_block = (block_ids[:, None] == block_ids[None, :]) & (
        positions[None, :] <= positions[:, None]
    )
    earlier_block = (block_ids[None, :] < block_ids[:, None]) & (spread_out > 0.5)
    return same_block | earlier_block


def add_states(first_term, second_term):
    return first_term + second_term


def shards(tokens, w_query, w_key, w_value, norm_gain, block_mask, cotangent):
    columns = w_query.shape[1]
    heads_here = columns // HDIM
    allowed = allowed_pairs(block_mask[0])
    seq_count = lax.axis_size("z") * lax.axis_size("core")
    fsdp_count = lax.axis_size("fsdp")
    weight_cat = gathered_by_exchange(
        jnp.concatenate([w_query, w_key, w_value], axis=1), SEQ, seq_count
    ).reshape(-1, 3 * columns)
    projected = jnp.dot(tokens, weight_cat, preferred_element_type=jnp.float32)
    projected = projected.astype(jnp.bfloat16)
    queries = projected[:, :columns].reshape(SEG, heads_here, HDIM)
    key_heads = projected[:, columns : 2 * columns].reshape(SEG, heads_here, HDIM)
    value_heads = projected[:, 2 * columns :].reshape(SEG, heads_here, HDIM)
    increment = jnp.einsum(
        "thd,the->hde", key_heads, value_heads, preferred_element_type=jnp.float32
    )
    state = entering_exchange(increment, SEQ, seq_count, False)
    state_low = state.astype(jnp.bfloat16)
    scores = jnp.einsum("shd,thd->hst", queries, key_heads, preferred_element_type=jnp.float32)
    weights = jnp.where(allowed[None], scores, 0.0).astype(jnp.bfloat16)
    mixed = jnp.einsum("shd,hde->she", queries, state_low, preferred_element_type=jnp.float32)
    mixed = mixed + jnp.einsum(
        "hst,the->she", weights, value_heads, preferred_element_type=jnp.float32
    )
    scale = lax.rsqrt(jnp.mean(mixed * mixed, axis=-1, keepdims=True) + EPSILON)
    normed = mixed * scale
    gain_heads = norm_gain.reshape(heads_here, HDIM)
    attended = (normed * gain_heads).reshape(SEG, columns).astype(jnp.bfloat16)
    given = cotangent.reshape(SEG, heads_here, HDIM).astype(jnp.float32) * gain_heads
    d_mixed = (scale * (given - normed * jnp.mean(given * normed, axis=-1, keepdims=True))).astype(
        jnp.bfloat16
    )
    d_state = jnp.einsum("shd,she->hde", queries, d_mixed, preferred_element_type=jnp.float32)
    later = entering(d_state, SEQ, seq_count, True)
    later_low = later.astype(jnp.bfloat16)
    d_scores = jnp.einsum("she,the->hst", d_mixed, value_heads, preferred_element_type=jnp.float32)
    d_weights = jnp.where(allowed[None], d_scores, 0.0).astype(jnp.bfloat16)
    d_queries = jnp.einsum("she,hde->shd", d_mixed, state_low, preferred_element_type=jnp.float32)
    d_queries = d_queries + jnp.einsum(
        "hst,thd->shd", d_weights, key_heads, preferred_element_type=jnp.float32
    )
    d_keys = jnp.einsum("hst,shd->thd", d_weights, queries, preferred_element_type=jnp.float32)
    d_keys = d_keys + jnp.einsum(
        "the,hde->thd", value_heads, later_low, preferred_element_type=jnp.float32
    )
    d_values = jnp.einsum("hst,she->the", weights, d_mixed, preferred_element_type=jnp.float32)
    d_values = d_values + jnp.einsum(
        "thd,hde->the", key_heads, later_low, preferred_element_type=jnp.float32
    )
    grad_cat = jnp.concatenate(
        [part.reshape(SEG, columns).astype(jnp.bfloat16) for part in (d_queries, d_keys, d_values)],
        axis=1,
    )
    input_rows = halving_scatter(
        lax.dot_general(
            weight_cat, grad_cat, (((1,), (1,)), ((), ())), preferred_element_type=jnp.float32
        ).astype(jnp.bfloat16),
        "fsdp",
        fsdp_count,
    )
    grad_tokens = input_rows.T.astype(jnp.bfloat16)
    weight_rows = halving_scatter(
        lax.dot_general(
            tokens, grad_cat, (((0,), (0,)), ((), ())), preferred_element_type=jnp.float32
        ).astype(jnp.bfloat16),
        SEQ,
        seq_count,
    )
    weight_rows = (weight_rows * (1.0 / math.sqrt(SEG * seq_count))).astype(jnp.bfloat16)
    return (
        attended,
        grad_tokens,
        weight_rows[:, :columns],
        weight_rows[:, columns : 2 * columns],
        weight_rows[:, 2 * columns :],
    )


def solution(mesh):
    split_mesh = Mesh(
        mesh.devices.reshape(mesh.shape["seq"] // 2, 2, mesh.shape["fsdp"]), ("z", "core", "fsdp")
    )
    placed = (
        P(SEQ, None),
        P(SEQ, "fsdp"),
        P(SEQ, "fsdp"),
        P(SEQ, "fsdp"),
        P("fsdp"),
        P(SEQ, None, None),
        P(SEQ, "fsdp"),
    )
    return jax.shard_map(
        shards,
        mesh=split_mesh,
        in_specs=placed,
        out_specs=(
            P(SEQ, "fsdp"),
            P(SEQ, "fsdp"),
            P(SEQ, "fsdp"),
            P(SEQ, "fsdp"),
            P(SEQ, "fsdp"),
        ),
        check_vma=False,
    )
```

```python
import math

import jax
import jax.numpy as jnp
from jax import lax
from jax.sharding import Mesh, PartitionSpec as P

HDIM = 128
BLOCK = 128
SEG = 384
NB = 3


EPSILON = 1e-06
SEQ = ("z", "core")


def entering(array, backward):
    count = lax.axis_size("z")
    core = lax.axis_index("core")
    partner = lax.ppermute(array, "core", [(0, 1), (1, 0)])
    pair_total = array + partner
    total = pair_total
    step = 1
    while step < count:
        parts = [total]
        for times in (1, 2, 3):
            shift = step * times
            if shift >= count:
                break
            if backward:
                pairs = [(i, i - shift) for i in range(shift, count)]
            else:
                pairs = [(i, i + shift) for i in range(count - shift)]
            parts.append(lax.ppermute(total, "z", pairs))
        total = sum(parts[1:], parts[0])
        step *= 4
    inside = jnp.where(core == (0 if backward else 1), partner, jnp.zeros_like(partner))
    return (total - pair_total) + inside


def halving_scatter(term, axis, count):
    place = lax.axis_index(axis)
    rows = term.shape[0] // count
    current = term.astype(jnp.float32).reshape(count, rows, term.shape[1])
    bit = 0
    while (1 << bit) < count:
        mine = (place >> bit) & 1
        split = current.reshape(current.shape[0] // 2, 2, rows, term.shape[1])
        keep = lax.dynamic_index_in_dim(split, mine, 1, False)
        away = lax.dynamic_index_in_dim(split, 1 - mine, 1, False)
        pairs = [(i, i ^ (1 << bit)) for i in range(count)]
        current = keep + lax.ppermute(away.astype(jnp.bfloat16), axis, pairs).astype(jnp.float32)
        bit += 1
    return current.reshape(rows, term.shape[1])


def allowed_pairs(pattern):
    positions = jnp.arange(SEG)
    block_ids = positions // BLOCK
    selector = (block_ids[:, None] == jnp.arange(NB)[None, :]).astype(jnp.float32)
    spread_out = jnp.dot(
        jnp.dot(selector, pattern.astype(jnp.float32), precision=lax.Precision.HIGHEST),
        selector.T,
        precision=lax.Precision.HIGHEST,
    )
    same_block = (block_ids[:, None] == block_ids[None, :]) & (
        positions[None, :] <= positions[:, None]
    )
    earlier_block = (block_ids[None, :] < block_ids[:, None]) & (spread_out > 0.5)
    return same_block | earlier_block


def add_states(first_term, second_term):
    return first_term + second_term


def shards(tokens, w_query, w_key, w_value, norm_gain, block_mask, cotangent):
    columns = w_query.shape[1]
    heads_here = columns // HDIM
    allowed = allowed_pairs(block_mask[0])
    seq_count = lax.axis_size("z") * lax.axis_size("core")
    fsdp_count = lax.axis_size("fsdp")
    pair_rows = lax.all_gather(
        jnp.concatenate([w_query, w_key, w_value], axis=1), "core", axis=0, tiled=True
    )
    weight_cat = lax.all_gather(pair_rows, "z", axis=0, tiled=True)
    projected = jnp.dot(tokens, weight_cat, preferred_element_type=jnp.float32)
    projected = projected.astype(jnp.bfloat16)
    queries = projected[:, :columns].reshape(SEG, heads_here, HDIM)
    key_heads = projected[:, columns : 2 * columns].reshape(SEG, heads_here, HDIM)
    value_heads = projected[:, 2 * columns :].reshape(SEG, heads_here, HDIM)
    increment = jnp.einsum(
        "thd,the->hde", key_heads, value_heads, preferred_element_type=jnp.float32
    )
    state = entering(increment, False)
    state_low = state.astype(jnp.bfloat16)
    scores = jnp.einsum("shd,thd->hst", queries, key_heads, preferred_element_type=jnp.float32)
    weights = jnp.where(allowed[None], scores, 0.0).astype(jnp.bfloat16)
    mixed = jnp.einsum("shd,hde->she", queries, state_low, preferred_element_type=jnp.float32)
    mixed = mixed + jnp.einsum(
        "hst,the->she", weights, value_heads, preferred_element_type=jnp.float32
    )
    scale = lax.rsqrt(jnp.mean(mixed * mixed, axis=-1, keepdims=True) + EPSILON)
    normed = mixed * scale
    gain_heads = norm_gain.reshape(heads_here, HDIM)
    attended = (normed * gain_heads).reshape(SEG, columns).astype(jnp.bfloat16)
    given = cotangent.reshape(SEG, heads_here, HDIM).astype(jnp.float32) * gain_heads
    d_mixed = (scale * (given - normed * jnp.mean(given * normed, axis=-1, keepdims=True))).astype(
        jnp.bfloat16
    )
    d_state = jnp.einsum("shd,she->hde", queries, d_mixed, preferred_element_type=jnp.float32)
    later = entering(d_state, True)
    later_low = later.astype(jnp.bfloat16)
    d_scores = jnp.einsum("she,the->hst", d_mixed, value_heads, preferred_element_type=jnp.float32)
    d_weights = jnp.where(allowed[None], d_scores, 0.0).astype(jnp.bfloat16)
    d_queries = jnp.einsum("she,hde->shd", d_mixed, state_low, preferred_element_type=jnp.float32)
    d_queries = d_queries + jnp.einsum(
        "hst,thd->shd", d_weights, key_heads, preferred_element_type=jnp.float32
    )
    d_keys = jnp.einsum("hst,shd->thd", d_weights, queries, preferred_element_type=jnp.float32)
    d_keys = d_keys + jnp.einsum(
        "the,hde->thd", value_heads, later_low, preferred_element_type=jnp.float32
    )
    d_values = jnp.einsum("hst,she->the", weights, d_mixed, preferred_element_type=jnp.float32)
    d_values = d_values + jnp.einsum(
        "thd,hde->the", key_heads, later_low, preferred_element_type=jnp.float32
    )
    grad_cat = jnp.concatenate(
        [part.reshape(SEG, columns).astype(jnp.bfloat16) for part in (d_queries, d_keys, d_values)],
        axis=1,
    )
    input_rows = halving_scatter(
        lax.dot_general(
            weight_cat, grad_cat, (((1,), (1,)), ((), ())), preferred_element_type=jnp.float32
        ).astype(jnp.bfloat16),
        "fsdp",
        fsdp_count,
    )
    grad_tokens = input_rows.T.astype(jnp.bfloat16)
    weight_rows = halving_scatter(
        lax.dot_general(
            tokens, grad_cat, (((0,), (0,)), ((), ())), preferred_element_type=jnp.float32
        ).astype(jnp.bfloat16),
        SEQ,
        seq_count,
    )
    weight_rows = (weight_rows * (1.0 / math.sqrt(SEG * seq_count))).astype(jnp.bfloat16)
    return (
        attended,
        grad_tokens,
        weight_rows[:, :columns],
        weight_rows[:, columns : 2 * columns],
        weight_rows[:, 2 * columns :],
    )


def solution(mesh):
    split_mesh = Mesh(
        mesh.devices.reshape(mesh.shape["seq"] // 2, 2, mesh.shape["fsdp"]), ("z", "core", "fsdp")
    )
    placed = (
        P(SEQ, None),
        P(SEQ, "fsdp"),
        P(SEQ, "fsdp"),
        P(SEQ, "fsdp"),
        P("fsdp"),
        P(SEQ, None, None),
        P(SEQ, "fsdp"),
    )
    return jax.shard_map(
        shards,
        mesh=split_mesh,
        in_specs=placed,
        out_specs=(
            P(SEQ, "fsdp"),
            P(SEQ, "fsdp"),
            P(SEQ, "fsdp"),
            P(SEQ, "fsdp"),
            P(SEQ, "fsdp"),
        ),
        check_vma=False,
    )
```

```python
import math

import jax
import jax.numpy as jnp
from jax import lax
from jax.sharding import Mesh, PartitionSpec as P

HDIM = 128
BLOCK = 128
SEG = 384
NB = 3


EPSILON = 1e-06
SEQ = ("z", "core")


def entering(array, backward):
    count = lax.axis_size("z")
    core = lax.axis_index("core")
    partner = lax.ppermute(array, "core", [(0, 1), (1, 0)])
    pair_total = array + partner
    total = pair_total
    step = 1
    while step < count:
        parts = [total]
        for times in (1, 2, 3):
            shift = step * times
            if shift >= count:
                break
            if backward:
                pairs = [(i, i - shift) for i in range(shift, count)]
            else:
                pairs = [(i, i + shift) for i in range(count - shift)]
            parts.append(lax.ppermute(total, "z", pairs))
        total = sum(parts[1:], parts[0])
        step *= 4
    inside = jnp.where(core == (0 if backward else 1), partner, jnp.zeros_like(partner))
    return (total - pair_total) + inside


def doubling_gather(block, axis, count):
    place = lax.axis_index(axis)
    current = block[None]
    bit = count.bit_length() - 2
    while bit >= 0:
        pairs = [(i, i ^ (1 << bit)) for i in range(count)]
        received = lax.ppermute(current, axis, pairs)
        upper = ((place >> bit) & 1) == 1
        low = jnp.where(upper, received, current)
        high = jnp.where(upper, current, received)
        current = jnp.stack([low, high], axis=1).reshape((-1,) + block.shape)
        bit -= 1
    return current


def halving_scatter(term, axis, count):
    place = lax.axis_index(axis)
    rows = term.shape[0] // count
    current = term.astype(jnp.float32).reshape(count, rows, term.shape[1])
    bit = 0
    while (1 << bit) < count:
        mine = (place >> bit) & 1
        split = current.reshape(current.shape[0] // 2, 2, rows, term.shape[1])
        keep = lax.dynamic_index_in_dim(split, mine, 1, False)
        away = lax.dynamic_index_in_dim(split, 1 - mine, 1, False)
        pairs = [(i, i ^ (1 << bit)) for i in range(count)]
        current = keep + lax.ppermute(away.astype(jnp.bfloat16), axis, pairs).astype(jnp.float32)
        bit += 1
    return current.reshape(rows, term.shape[1])


def allowed_pairs(pattern):
    positions = jnp.arange(SEG)
    block_ids = positions // BLOCK
    selector = (block_ids[:, None] == jnp.arange(NB)[None, :]).astype(jnp.float32)
    spread_out = jnp.dot(
        jnp.dot(selector, pattern.astype(jnp.float32), precision=lax.Precision.HIGHEST),
        selector.T,
        precision=lax.Precision.HIGHEST,
    )
    same_block = (block_ids[:, None] == block_ids[None, :]) & (
        positions[None, :] <= positions[:, None]
    )
    earlier_block = (block_ids[None, :] < block_ids[:, None]) & (spread_out > 0.5)
    return same_block | earlier_block


def add_states(first_term, second_term):
    return first_term + second_term


def shards(tokens, w_query, w_key, w_value, norm_gain, block_mask, cotangent):
    columns = w_query.shape[1]
    heads_here = columns // HDIM
    allowed = allowed_pairs(block_mask[0])
    seq_count = lax.axis_size("z") * lax.axis_size("core")
    fsdp_count = lax.axis_size("fsdp")
    own_rows = jnp.concatenate([w_query, w_key, w_value], axis=1)
    chip_rows = doubling_gather(own_rows, "z", lax.axis_size("z"))
    other_rows = lax.ppermute(chip_rows, "core", [(0, 1), (1, 0)])
    second_core = lax.axis_index("core") == 1
    weight_cat = jnp.stack(
        [
            jnp.where(second_core, other_rows, chip_rows),
            jnp.where(second_core, chip_rows, other_rows),
        ],
        axis=1,
    ).reshape(-1, 3 * columns)
    projected = jnp.dot(tokens, weight_cat, preferred_element_type=jnp.float32)
    projected = projected.astype(jnp.bfloat16)
    queries = projected[:, :columns].reshape(SEG, heads_here, HDIM)
    key_heads = projected[:, columns : 2 * columns].reshape(SEG, heads_here, HDIM)
    value_heads = projected[:, 2 * columns :].reshape(SEG, heads_here, HDIM)
    increment = jnp.einsum(
        "thd,the->hde", key_heads, value_heads, preferred_element_type=jnp.float32
    )
    state = entering(increment, False)
    state_low = state.astype(jnp.bfloat16)
    scores = jnp.einsum("shd,thd->hst", queries, key_heads, preferred_element_type=jnp.float32)
    weights = jnp.where(allowed[None], scores, 0.0).astype(jnp.bfloat16)
    mixed = jnp.einsum("shd,hde->she", queries, state_low, preferred_element_type=jnp.float32)
    mixed = mixed + jnp.einsum(
        "hst,the->she", weights, value_heads, preferred_element_type=jnp.float32
    )
    scale = lax.rsqrt(jnp.mean(mixed * mixed, axis=-1, keepdims=True) + EPSILON)
    normed = mixed * scale
    gain_heads = norm_gain.reshape(heads_here, HDIM)
    attended = (normed * gain_heads).reshape(SEG, columns).astype(jnp.bfloat16)
    given = cotangent.reshape(SEG, heads_here, HDIM).astype(jnp.float32) * gain_heads
    d_mixed = (scale * (given - normed * jnp.mean(given * normed, axis=-1, keepdims=True))).astype(
        jnp.bfloat16
    )
    d_state = jnp.einsum("shd,she->hde", queries, d_mixed, preferred_element_type=jnp.float32)
    later = entering(d_state, True)
    later_low = later.astype(jnp.bfloat16)
    d_scores = jnp.einsum("she,the->hst", d_mixed, value_heads, preferred_element_type=jnp.float32)
    d_weights = jnp.where(allowed[None], d_scores, 0.0).astype(jnp.bfloat16)
    d_queries = jnp.einsum("she,hde->shd", d_mixed, state_low, preferred_element_type=jnp.float32)
    d_queries = d_queries + jnp.einsum(
        "hst,thd->shd", d_weights, key_heads, preferred_element_type=jnp.float32
    )
    d_keys = jnp.einsum("hst,shd->thd", d_weights, queries, preferred_element_type=jnp.float32)
    d_keys = d_keys + jnp.einsum(
        "the,hde->thd", value_heads, later_low, preferred_element_type=jnp.float32
    )
    d_values = jnp.einsum("hst,she->the", weights, d_mixed, preferred_element_type=jnp.float32)
    d_values = d_values + jnp.einsum(
        "thd,hde->the", key_heads, later_low, preferred_element_type=jnp.float32
    )
    grad_cat = jnp.concatenate(
        [part.reshape(SEG, columns).astype(jnp.bfloat16) for part in (d_queries, d_keys, d_values)],
        axis=1,
    )
    input_rows = halving_scatter(
        lax.dot_general(
            weight_cat, grad_cat, (((1,), (1,)), ((), ())), preferred_element_type=jnp.float32
        ).astype(jnp.bfloat16),
        "fsdp",
        fsdp_count,
    )
    grad_tokens = input_rows.T.astype(jnp.bfloat16)
    weight_rows = halving_scatter(
        lax.dot_general(
            tokens, grad_cat, (((0,), (0,)), ((), ())), preferred_element_type=jnp.float32
        ).astype(jnp.bfloat16),
        SEQ,
        seq_count,
    )
    weight_rows = (weight_rows * (1.0 / math.sqrt(SEG * seq_count))).astype(jnp.bfloat16)
    return (
        attended,
        grad_tokens,
        weight_rows[:, :columns],
        weight_rows[:, columns : 2 * columns],
        weight_rows[:, 2 * columns :],
    )


def solution(mesh):
    split_mesh = Mesh(
        mesh.devices.reshape(mesh.shape["seq"] // 2, 2, mesh.shape["fsdp"]), ("z", "core", "fsdp")
    )
    placed = (
        P(SEQ, None),
        P(SEQ, "fsdp"),
        P(SEQ, "fsdp"),
        P(SEQ, "fsdp"),
        P("fsdp"),
        P(SEQ, None, None),
        P(SEQ, "fsdp"),
    )
    return jax.shard_map(
        shards,
        mesh=split_mesh,
        in_specs=placed,
        out_specs=(
            P(SEQ, "fsdp"),
            P(SEQ, "fsdp"),
            P(SEQ, "fsdp"),
            P(SEQ, "fsdp"),
            P(SEQ, "fsdp"),
        ),
        check_vma=False,
    )
```

```python
import math

import jax
import jax.numpy as jnp
from jax import lax
from jax.sharding import Mesh, PartitionSpec as P

HDIM = 128
BLOCK = 128
SEG = 384
NB = 3


EPSILON = 1e-06
SEQ = ("z", "core")


def entering(array, backward):
    count = lax.axis_size("z")
    core = lax.axis_index("core")
    partner = lax.ppermute(array, "core", [(0, 1), (1, 0)])
    pair_total = array + partner
    total = pair_total
    step = 1
    while step < count:
        parts = [total]
        for times in (1, 2, 3):
            shift = step * times
            if shift >= count:
                break
            if backward:
                pairs = [(i, i - shift) for i in range(shift, count)]
            else:
                pairs = [(i, i + shift) for i in range(count - shift)]
            parts.append(lax.ppermute(total, "z", pairs))
        total = sum(parts[1:], parts[0])
        step *= 4
    inside = jnp.where(core == (0 if backward else 1), partner, jnp.zeros_like(partner))
    return (total - pair_total) + inside


def doubling_gather(block, axis, count):
    place = lax.axis_index(axis)
    current = block[None]
    bit = count.bit_length() - 2
    while bit >= 0:
        pairs = [(i, i ^ (1 << bit)) for i in range(count)]
        received = lax.ppermute(current, axis, pairs)
        upper = ((place >> bit) & 1) == 1
        low = jnp.where(upper, received, current)
        high = jnp.where(upper, current, received)
        current = jnp.stack([low, high], axis=1).reshape((-1,) + block.shape)
        bit -= 1
    return current


def radices_for(count):
    radices = []
    while count % 4 == 0:
        radices.append(4)
        count //= 4
    if count > 1:
        radices.append(count)
    return tuple(radices)


def digit_pairs(count, stride, radix, offset):
    pairs = []
    for i in range(count):
        digit = (i // stride) % radix
        pairs.append((i, i + ((digit + offset) % radix - digit) * stride))
    return pairs


def exchange_gather(block, axis, radices):
    count = math.prod(radices)
    place = lax.axis_index(axis)
    strides = [math.prod(radices[:k]) for k in range(len(radices))]
    current = block[None]
    for radix, stride in reversed(list(zip(radices, strides))):
        digit = (place // stride) % radix
        got = [current]
        for offset in range(1, radix):
            got.append(lax.ppermute(current, axis, digit_pairs(count, stride, radix, offset)))
        blocks = []
        for value in range(radix):
            pick = got[0]
            for offset in range(1, radix):
                pick = jnp.where((digit - value) % radix == offset, got[offset], pick)
            blocks.append(pick)
        current = jnp.stack(blocks, axis=1).reshape((-1,) + block.shape)
    return current


def exchange_scatter(term, axis, radices):
    count = math.prod(radices)
    place = lax.axis_index(axis)
    rows = term.shape[0] // count
    cols = term.shape[1]
    current = term.astype(jnp.float32).reshape(count, rows, cols)
    stride = 1
    for radix in radices:
        digit = (place // stride) % radix
        split = current.reshape(-1, radix, rows, cols)
        total = lax.dynamic_index_in_dim(split, digit, 1, False)
        for offset in range(1, radix):
            away = lax.dynamic_index_in_dim(split, (digit + offset) % radix, 1, False)
            moved = lax.ppermute(
                away.astype(jnp.bfloat16), axis, digit_pairs(count, stride, radix, offset)
            )
            total = total + moved.astype(jnp.float32)
        current = total
        stride *= radix
    return current.reshape(rows, cols)


def halving_scatter(term, axis, count):
    place = lax.axis_index(axis)
    rows = term.shape[0] // count
    current = term.astype(jnp.float32).reshape(count, rows, term.shape[1])
    bit = 0
    while (1 << bit) < count:
        mine = (place >> bit) & 1
        split = current.reshape(current.shape[0] // 2, 2, rows, term.shape[1])
        keep = lax.dynamic_index_in_dim(split, mine, 1, False)
        away = lax.dynamic_index_in_dim(split, 1 - mine, 1, False)
        pairs = [(i, i ^ (1 << bit)) for i in range(count)]
        current = keep + lax.ppermute(away.astype(jnp.bfloat16), axis, pairs).astype(jnp.float32)
        bit += 1
    return current.reshape(rows, term.shape[1])


def allowed_pairs(pattern):
    positions = jnp.arange(SEG)
    block_ids = positions // BLOCK
    selector = (block_ids[:, None] == jnp.arange(NB)[None, :]).astype(jnp.float32)
    spread_out = jnp.dot(
        jnp.dot(selector, pattern.astype(jnp.float32), precision=lax.Precision.HIGHEST),
        selector.T,
        precision=lax.Precision.HIGHEST,
    )
    same_block = (block_ids[:, None] == block_ids[None, :]) & (
        positions[None, :] <= positions[:, None]
    )
    earlier_block = (block_ids[None, :] < block_ids[:, None]) & (spread_out > 0.5)
    return same_block | earlier_block


def add_states(first_term, second_term):
    return first_term + second_term


def shards(tokens, w_query, w_key, w_value, norm_gain, block_mask, cotangent):
    columns = w_query.shape[1]
    heads_here = columns // HDIM
    allowed = allowed_pairs(block_mask[0])
    seq_count = lax.axis_size("z") * lax.axis_size("core")
    fsdp_count = lax.axis_size("fsdp")
    seq_radices = (lax.axis_size("core"),) + radices_for(lax.axis_size("z"))
    fsdp_radices = radices_for(fsdp_count)
    weight_cat = exchange_gather(
        jnp.concatenate([w_query, w_key, w_value], axis=1), SEQ, seq_radices
    ).reshape(-1, 3 * columns)
    projected = jnp.dot(tokens, weight_cat, preferred_element_type=jnp.float32)
    projected = projected.astype(jnp.bfloat16)
    queries = projected[:, :columns].reshape(SEG, heads_here, HDIM)
    key_heads = projected[:, columns : 2 * columns].reshape(SEG, heads_here, HDIM)
    value_heads = projected[:, 2 * columns :].reshape(SEG, heads_here, HDIM)
    increment = jnp.einsum(
        "thd,the->hde", key_heads, value_heads, preferred_element_type=jnp.float32
    )
    state = entering(increment, False)
    state_low = state.astype(jnp.bfloat16)
    scores = jnp.einsum("shd,thd->hst", queries, key_heads, preferred_element_type=jnp.float32)
    weights = jnp.where(allowed[None], scores, 0.0).astype(jnp.bfloat16)
    mixed = jnp.einsum("shd,hde->she", queries, state_low, preferred_element_type=jnp.float32)
    mixed = mixed + jnp.einsum(
        "hst,the->she", weights, value_heads, preferred_element_type=jnp.float32
    )
    scale = lax.rsqrt(jnp.mean(mixed * mixed, axis=-1, keepdims=True) + EPSILON)
    normed = mixed * scale
    gain_heads = norm_gain.reshape(heads_here, HDIM)
    attended = (normed * gain_heads).reshape(SEG, columns).astype(jnp.bfloat16)
    given = cotangent.reshape(SEG, heads_here, HDIM).astype(jnp.float32) * gain_heads
    d_mixed = (scale * (given - normed * jnp.mean(given * normed, axis=-1, keepdims=True))).astype(
        jnp.bfloat16
    )
    d_state = jnp.einsum("shd,she->hde", queries, d_mixed, preferred_element_type=jnp.float32)
    later = entering(d_state, True)
    later_low = later.astype(jnp.bfloat16)
    d_scores = jnp.einsum("she,the->hst", d_mixed, value_heads, preferred_element_type=jnp.float32)
    d_weights = jnp.where(allowed[None], d_scores, 0.0).astype(jnp.bfloat16)
    d_queries = jnp.einsum("she,hde->shd", d_mixed, state_low, preferred_element_type=jnp.float32)
    d_queries = d_queries + jnp.einsum(
        "hst,thd->shd", d_weights, key_heads, preferred_element_type=jnp.float32
    )
    d_keys = jnp.einsum("hst,shd->thd", d_weights, queries, preferred_element_type=jnp.float32)
    d_keys = d_keys + jnp.einsum(
        "the,hde->thd", value_heads, later_low, preferred_element_type=jnp.float32
    )
    d_values = jnp.einsum("hst,she->the", weights, d_mixed, preferred_element_type=jnp.float32)
    d_values = d_values + jnp.einsum(
        "thd,hde->the", key_heads, later_low, preferred_element_type=jnp.float32
    )
    grad_cat = jnp.concatenate(
        [part.reshape(SEG, columns).astype(jnp.bfloat16) for part in (d_queries, d_keys, d_values)],
        axis=1,
    )
    input_rows = exchange_scatter(
        lax.dot_general(
            weight_cat, grad_cat, (((1,), (1,)), ((), ())), preferred_element_type=jnp.float32
        ).astype(jnp.bfloat16),
        "fsdp",
        fsdp_radices,
    )
    grad_tokens = input_rows.T.astype(jnp.bfloat16)
    weight_rows = exchange_scatter(
        lax.dot_general(
            tokens, grad_cat, (((0,), (0,)), ((), ())), preferred_element_type=jnp.float32
        ).astype(jnp.bfloat16),
        SEQ,
        seq_radices,
    )
    weight_rows = (weight_rows * (1.0 / math.sqrt(SEG * seq_count))).astype(jnp.bfloat16)
    return (
        attended,
        grad_tokens,
        weight_rows[:, :columns],
        weight_rows[:, columns : 2 * columns],
        weight_rows[:, 2 * columns :],
    )


def solution(mesh):
    split_mesh = Mesh(
        mesh.devices.reshape(mesh.shape["seq"] // 2, 2, mesh.shape["fsdp"]), ("z", "core", "fsdp")
    )
    placed = (
        P(SEQ, None),
        P(SEQ, "fsdp"),
        P(SEQ, "fsdp"),
        P(SEQ, "fsdp"),
        P("fsdp"),
        P(SEQ, None, None),
        P(SEQ, "fsdp"),
    )
    return jax.shard_map(
        shards,
        mesh=split_mesh,
        in_specs=placed,
        out_specs=(
            P(SEQ, "fsdp"),
            P(SEQ, "fsdp"),
            P(SEQ, "fsdp"),
            P(SEQ, "fsdp"),
            P(SEQ, "fsdp"),
        ),
        check_vma=False,
    )
```

```python
import math

import jax
import jax.numpy as jnp
from jax import lax
from jax.sharding import Mesh, PartitionSpec as P

HDIM = 128
BLOCK = 128
SEG = 384
NB = 3


EPSILON = 1e-06
SEQ = ("z", "core")


def entering(array, backward):
    count = lax.axis_size("z")
    core = lax.axis_index("core")
    partner = lax.ppermute(array, "core", [(0, 1), (1, 0)])
    pair_total = array + partner
    total = pair_total
    step = 1
    while step < count:
        parts = [total]
        for times in (1, 2, 3):
            shift = step * times
            if shift >= count:
                break
            if backward:
                pairs = [(i, i - shift) for i in range(shift, count)]
            else:
                pairs = [(i, i + shift) for i in range(count - shift)]
            parts.append(lax.ppermute(total, "z", pairs))
        total = sum(parts[1:], parts[0])
        step *= 4
    inside = jnp.where(core == (0 if backward else 1), partner, jnp.zeros_like(partner))
    return (total - pair_total) + inside


def doubling_gather(block, axis, count):
    place = lax.axis_index(axis)
    current = block[None]
    bit = count.bit_length() - 2
    while bit >= 0:
        pairs = [(i, i ^ (1 << bit)) for i in range(count)]
        received = lax.ppermute(current, axis, pairs)
        upper = ((place >> bit) & 1) == 1
        low = jnp.where(upper, received, current)
        high = jnp.where(upper, current, received)
        current = jnp.stack([low, high], axis=1).reshape((-1,) + block.shape)
        bit -= 1
    return current


def radices_for(count):
    radices = []
    while count % 4 == 0:
        radices.append(4)
        count //= 4
    if count > 1:
        radices.append(count)
    return tuple(radices)


def digit_pairs(count, stride, radix, offset):
    pairs = []
    for i in range(count):
        digit = (i // stride) % radix
        pairs.append((i, i + ((digit + offset) % radix - digit) * stride))
    return pairs


def exchange_gather(block, axis, radices):
    count = math.prod(radices)
    place = lax.axis_index(axis)
    strides = [math.prod(radices[:k]) for k in range(len(radices))]
    current = block[None]
    for radix, stride in reversed(list(zip(radices, strides))):
        digit = (place // stride) % radix
        got = [current]
        for offset in range(1, radix):
            got.append(lax.ppermute(current, axis, digit_pairs(count, stride, radix, offset)))
        blocks = []
        for value in range(radix):
            pick = got[0]
            for offset in range(1, radix):
                pick = jnp.where((digit - value) % radix == offset, got[offset], pick)
            blocks.append(pick)
        current = jnp.stack(blocks, axis=1).reshape((-1,) + block.shape)
    return current


def exchange_scatter(term, axis, radices):
    count = math.prod(radices)
    place = lax.axis_index(axis)
    rows = term.shape[0] // count
    cols = term.shape[1]
    current = term.reshape(count, rows, cols)
    stride = 1
    for radix in radices:
        digit = (place // stride) % radix
        split = current.reshape(-1, radix, rows, cols)
        total = lax.dynamic_index_in_dim(split, digit, 1, False).astype(jnp.float32)
        for offset in range(1, radix):
            away = lax.dynamic_index_in_dim(split, (digit + offset) % radix, 1, False)
            moved = lax.ppermute(
                away.astype(jnp.bfloat16), axis, digit_pairs(count, stride, radix, offset)
            )
            total = total + moved.astype(jnp.float32)
        current = total
        stride *= radix
    return current.reshape(rows, cols)


def halving_scatter(term, axis, count):
    place = lax.axis_index(axis)
    rows = term.shape[0] // count
    current = term.astype(jnp.float32).reshape(count, rows, term.shape[1])
    bit = 0
    while (1 << bit) < count:
        mine = (place >> bit) & 1
        split = current.reshape(current.shape[0] // 2, 2, rows, term.shape[1])
        keep = lax.dynamic_index_in_dim(split, mine, 1, False)
        away = lax.dynamic_index_in_dim(split, 1 - mine, 1, False)
        pairs = [(i, i ^ (1 << bit)) for i in range(count)]
        current = keep + lax.ppermute(away.astype(jnp.bfloat16), axis, pairs).astype(jnp.float32)
        bit += 1
    return current.reshape(rows, term.shape[1])


def allowed_pairs(pattern):
    positions = jnp.arange(SEG)
    block_ids = positions // BLOCK
    selector = (block_ids[:, None] == jnp.arange(NB)[None, :]).astype(jnp.float32)
    spread_out = jnp.dot(
        jnp.dot(selector, pattern.astype(jnp.float32), precision=lax.Precision.HIGHEST),
        selector.T,
        precision=lax.Precision.HIGHEST,
    )
    same_block = (block_ids[:, None] == block_ids[None, :]) & (
        positions[None, :] <= positions[:, None]
    )
    earlier_block = (block_ids[None, :] < block_ids[:, None]) & (spread_out > 0.5)
    return same_block | earlier_block


def add_states(first_term, second_term):
    return first_term + second_term


def shards(tokens, w_query, w_key, w_value, norm_gain, block_mask, cotangent):
    columns = w_query.shape[1]
    heads_here = columns // HDIM
    allowed = allowed_pairs(block_mask[0])
    seq_count = lax.axis_size("z") * lax.axis_size("core")
    fsdp_count = lax.axis_size("fsdp")
    seq_radices = (lax.axis_size("core"),) + radices_for(lax.axis_size("z"))
    fsdp_radices = radices_for(fsdp_count)
    weight_cat = exchange_gather(
        jnp.concatenate([w_query, w_key, w_value], axis=1), SEQ, seq_radices
    ).reshape(-1, 3 * columns)
    projected = jnp.dot(tokens, weight_cat, preferred_element_type=jnp.float32)
    projected = projected.astype(jnp.bfloat16)
    queries = projected[:, :columns].reshape(SEG, heads_here, HDIM)
    key_heads = projected[:, columns : 2 * columns].reshape(SEG, heads_here, HDIM)
    value_heads = projected[:, 2 * columns :].reshape(SEG, heads_here, HDIM)
    increment = jnp.einsum(
        "thd,the->hde", key_heads, value_heads, preferred_element_type=jnp.float32
    )
    state = entering(increment, False)
    state_low = state.astype(jnp.bfloat16)
    scores = jnp.einsum("shd,thd->hst", queries, key_heads, preferred_element_type=jnp.float32)
    weights = jnp.where(allowed[None], scores, 0.0).astype(jnp.bfloat16)
    mixed = jnp.einsum("shd,hde->she", queries, state_low, preferred_element_type=jnp.float32)
    mixed = mixed + jnp.einsum(
        "hst,the->she", weights, value_heads, preferred_element_type=jnp.float32
    )
    scale = lax.rsqrt(jnp.mean(mixed * mixed, axis=-1, keepdims=True) + EPSILON)
    normed = mixed * scale
    gain_heads = norm_gain.reshape(heads_here, HDIM)
    attended = (normed * gain_heads).reshape(SEG, columns).astype(jnp.bfloat16)
    given = cotangent.reshape(SEG, heads_here, HDIM).astype(jnp.float32) * gain_heads
    d_mixed = (scale * (given - normed * jnp.mean(given * normed, axis=-1, keepdims=True))).astype(
        jnp.bfloat16
    )
    d_state = jnp.einsum("shd,she->hde", queries, d_mixed, preferred_element_type=jnp.float32)
    later = entering(d_state, True)
    later_low = later.astype(jnp.bfloat16)
    d_scores = jnp.einsum("she,the->hst", d_mixed, value_heads, preferred_element_type=jnp.float32)
    d_weights = jnp.where(allowed[None], d_scores, 0.0).astype(jnp.bfloat16)
    d_queries = jnp.einsum("she,hde->shd", d_mixed, state_low, preferred_element_type=jnp.float32)
    d_queries = d_queries + jnp.einsum(
        "hst,thd->shd", d_weights, key_heads, preferred_element_type=jnp.float32
    )
    d_keys = jnp.einsum("hst,shd->thd", d_weights, queries, preferred_element_type=jnp.float32)
    d_keys = d_keys + jnp.einsum(
        "the,hde->thd", value_heads, later_low, preferred_element_type=jnp.float32
    )
    d_values = jnp.einsum("hst,she->the", weights, d_mixed, preferred_element_type=jnp.float32)
    d_values = d_values + jnp.einsum(
        "thd,hde->the", key_heads, later_low, preferred_element_type=jnp.float32
    )
    grad_cat = jnp.concatenate(
        [part.reshape(SEG, columns).astype(jnp.bfloat16) for part in (d_queries, d_keys, d_values)],
        axis=1,
    )
    input_rows = exchange_scatter(
        lax.dot_general(
            weight_cat, grad_cat, (((1,), (1,)), ((), ())), preferred_element_type=jnp.float32
        ).astype(jnp.bfloat16),
        "fsdp",
        fsdp_radices,
    )
    grad_tokens = input_rows.T.astype(jnp.bfloat16)
    weight_rows = exchange_scatter(
        lax.dot_general(
            tokens, grad_cat, (((0,), (0,)), ((), ())), preferred_element_type=jnp.float32
        ).astype(jnp.bfloat16),
        SEQ,
        seq_radices,
    )
    weight_rows = (weight_rows * (1.0 / math.sqrt(SEG * seq_count))).astype(jnp.bfloat16)
    return (
        attended,
        grad_tokens,
        weight_rows[:, :columns],
        weight_rows[:, columns : 2 * columns],
        weight_rows[:, 2 * columns :],
    )


def solution(mesh):
    split_mesh = Mesh(
        mesh.devices.reshape(mesh.shape["seq"] // 2, 2, mesh.shape["fsdp"]), ("z", "core", "fsdp")
    )
    placed = (
        P(SEQ, None),
        P(SEQ, "fsdp"),
        P(SEQ, "fsdp"),
        P(SEQ, "fsdp"),
        P("fsdp"),
        P(SEQ, None, None),
        P(SEQ, "fsdp"),
    )
    return jax.shard_map(
        shards,
        mesh=split_mesh,
        in_specs=placed,
        out_specs=(
            P(SEQ, "fsdp"),
            P(SEQ, "fsdp"),
            P(SEQ, "fsdp"),
            P(SEQ, "fsdp"),
            P(SEQ, "fsdp"),
        ),
        check_vma=False,
    )
```

```python
import math

import jax
import jax.numpy as jnp
from jax import lax
from jax.sharding import Mesh, PartitionSpec as P

HDIM = 128
BLOCK = 128
SEG = 384
NB = 3


EPSILON = 1e-06
SEQ = ("z", "core")


def entering(array, backward):
    count = lax.axis_size("z")
    core = lax.axis_index("core")
    partner = lax.ppermute(array, "core", [(0, 1), (1, 0)])
    pair_total = array + partner
    total = pair_total
    step = 1
    while step < count:
        parts = [total]
        for times in (1, 2, 3):
            shift = step * times
            if shift >= count:
                break
            if backward:
                pairs = [(i, i - shift) for i in range(shift, count)]
            else:
                pairs = [(i, i + shift) for i in range(count - shift)]
            parts.append(lax.ppermute(total, "z", pairs))
        total = sum(parts[1:], parts[0])
        step *= 4
    inside = jnp.where(core == (0 if backward else 1), partner, jnp.zeros_like(partner))
    return (total - pair_total) + inside


def doubling_gather(block, axis, count):
    place = lax.axis_index(axis)
    current = block[None]
    bit = count.bit_length() - 2
    while bit >= 0:
        pairs = [(i, i ^ (1 << bit)) for i in range(count)]
        received = lax.ppermute(current, axis, pairs)
        upper = ((place >> bit) & 1) == 1
        low = jnp.where(upper, received, current)
        high = jnp.where(upper, current, received)
        current = jnp.stack([low, high], axis=1).reshape((-1,) + block.shape)
        bit -= 1
    return current


def radices_for(count):
    radices = []
    while count % 4 == 0:
        radices.append(4)
        count //= 4
    if count > 1:
        radices.append(count)
    return tuple(radices)


def digit_pairs(count, stride, radix, offset):
    pairs = []
    for i in range(count):
        digit = (i // stride) % radix
        pairs.append((i, i + ((digit + offset) % radix - digit) * stride))
    return pairs


def exchange_gather(block, axis, radices):
    count = math.prod(radices)
    place = lax.axis_index(axis)
    strides = [math.prod(radices[:k]) for k in range(len(radices))]
    current = block[None]
    for radix, stride in reversed(list(zip(radices, strides))):
        digit = (place // stride) % radix
        got = [current]
        for offset in range(1, radix):
            got.append(lax.ppermute(current, axis, digit_pairs(count, stride, radix, offset)))
        blocks = []
        for value in range(radix):
            pick = got[0]
            for offset in range(1, radix):
                pick = jnp.where((digit - value) % radix == offset, got[offset], pick)
            blocks.append(pick)
        current = jnp.stack(blocks, axis=1).reshape((-1,) + block.shape)
    return current


def exchange_scatter(term, axis, radices):
    count = math.prod(radices)
    place = lax.axis_index(axis)
    rows = term.shape[0] // count
    cols = term.shape[1]
    current = term.reshape(count, rows, cols)
    stride = 1
    for radix in radices:
        digit = (place // stride) % radix
        split = current.reshape(-1, radix, rows, cols)
        total = lax.dynamic_index_in_dim(split, digit, 1, False).astype(jnp.float32)
        for offset in range(1, radix):
            away = lax.dynamic_index_in_dim(split, (digit + offset) % radix, 1, False)
            moved = lax.ppermute(
                away.astype(jnp.bfloat16), axis, digit_pairs(count, stride, radix, offset)
            )
            total = total + moved.astype(jnp.float32)
        current = total
        stride *= radix
    return current.reshape(rows, cols)


def halving_scatter(term, axis, count):
    place = lax.axis_index(axis)
    rows = term.shape[0] // count
    current = term.astype(jnp.float32).reshape(count, rows, term.shape[1])
    bit = 0
    while (1 << bit) < count:
        mine = (place >> bit) & 1
        split = current.reshape(current.shape[0] // 2, 2, rows, term.shape[1])
        keep = lax.dynamic_index_in_dim(split, mine, 1, False)
        away = lax.dynamic_index_in_dim(split, 1 - mine, 1, False)
        pairs = [(i, i ^ (1 << bit)) for i in range(count)]
        current = keep + lax.ppermute(away.astype(jnp.bfloat16), axis, pairs).astype(jnp.float32)
        bit += 1
    return current.reshape(rows, term.shape[1])


def allowed_pairs(pattern):
    positions = jnp.arange(SEG)
    block_ids = positions // BLOCK
    selector = (block_ids[:, None] == jnp.arange(NB)[None, :]).astype(jnp.float32)
    spread_out = jnp.dot(
        jnp.dot(selector, pattern.astype(jnp.float32), precision=lax.Precision.HIGHEST),
        selector.T,
        precision=lax.Precision.HIGHEST,
    )
    same_block = (block_ids[:, None] == block_ids[None, :]) & (
        positions[None, :] <= positions[:, None]
    )
    earlier_block = (block_ids[None, :] < block_ids[:, None]) & (spread_out > 0.5)
    return same_block | earlier_block


def add_states(first_term, second_term):
    return first_term + second_term


def shards(tokens, w_query, w_key, w_value, norm_gain, block_mask, cotangent):
    columns = w_query.shape[1]
    heads_here = columns // HDIM
    allowed = allowed_pairs(block_mask[0])
    seq_count = lax.axis_size("z") * lax.axis_size("core")
    fsdp_count = lax.axis_size("fsdp")
    seq_radices = (lax.axis_size("core"),) + radices_for(lax.axis_size("z"))
    fsdp_radices = radices_for(fsdp_count)
    pair_cat = exchange_gather(
        jnp.concatenate([w_key, w_value], axis=1), SEQ, seq_radices
    ).reshape(-1, 2 * columns)
    pair_projected = jnp.dot(tokens, pair_cat, preferred_element_type=jnp.float32)
    pair_projected = pair_projected.astype(jnp.bfloat16)
    key_heads = pair_projected[:, :columns].reshape(SEG, heads_here, HDIM)
    value_heads = pair_projected[:, columns:].reshape(SEG, heads_here, HDIM)
    increment = jnp.einsum(
        "thd,the->hde", key_heads, value_heads, preferred_element_type=jnp.float32
    )
    query_rows, increment = lax.optimization_barrier((w_query, increment))
    query_cat = exchange_gather(query_rows, SEQ, seq_radices).reshape(-1, columns)
    queries = jnp.dot(tokens, query_cat, preferred_element_type=jnp.float32)
    queries = queries.astype(jnp.bfloat16).reshape(SEG, heads_here, HDIM)
    weight_cat = jnp.concatenate([query_cat, pair_cat], axis=1)
    state = entering(increment, False)
    state_low = state.astype(jnp.bfloat16)
    scores = jnp.einsum("shd,thd->hst", queries, key_heads, preferred_element_type=jnp.float32)
    weights = jnp.where(allowed[None], scores, 0.0).astype(jnp.bfloat16)
    mixed = jnp.einsum("shd,hde->she", queries, state_low, preferred_element_type=jnp.float32)
    mixed = mixed + jnp.einsum(
        "hst,the->she", weights, value_heads, preferred_element_type=jnp.float32
    )
    scale = lax.rsqrt(jnp.mean(mixed * mixed, axis=-1, keepdims=True) + EPSILON)
    normed = mixed * scale
    gain_heads = norm_gain.reshape(heads_here, HDIM)
    attended = (normed * gain_heads).reshape(SEG, columns).astype(jnp.bfloat16)
    given = cotangent.reshape(SEG, heads_here, HDIM).astype(jnp.float32) * gain_heads
    d_mixed = (scale * (given - normed * jnp.mean(given * normed, axis=-1, keepdims=True))).astype(
        jnp.bfloat16
    )
    d_state = jnp.einsum("shd,she->hde", queries, d_mixed, preferred_element_type=jnp.float32)
    later = entering(d_state, True)
    later_low = later.astype(jnp.bfloat16)
    d_scores = jnp.einsum("she,the->hst", d_mixed, value_heads, preferred_element_type=jnp.float32)
    d_weights = jnp.where(allowed[None], d_scores, 0.0).astype(jnp.bfloat16)
    d_queries = jnp.einsum("she,hde->shd", d_mixed, state_low, preferred_element_type=jnp.float32)
    d_queries = d_queries + jnp.einsum(
        "hst,thd->shd", d_weights, key_heads, preferred_element_type=jnp.float32
    )
    d_keys = jnp.einsum("hst,shd->thd", d_weights, queries, preferred_element_type=jnp.float32)
    d_keys = d_keys + jnp.einsum(
        "the,hde->thd", value_heads, later_low, preferred_element_type=jnp.float32
    )
    d_values = jnp.einsum("hst,she->the", weights, d_mixed, preferred_element_type=jnp.float32)
    d_values = d_values + jnp.einsum(
        "thd,hde->the", key_heads, later_low, preferred_element_type=jnp.float32
    )
    grad_cat = jnp.concatenate(
        [part.reshape(SEG, columns).astype(jnp.bfloat16) for part in (d_queries, d_keys, d_values)],
        axis=1,
    )
    input_rows = exchange_scatter(
        lax.dot_general(
            weight_cat, grad_cat, (((1,), (1,)), ((), ())), preferred_element_type=jnp.float32
        ).astype(jnp.bfloat16),
        "fsdp",
        fsdp_radices,
    )
    grad_tokens = input_rows.T.astype(jnp.bfloat16)
    weight_rows = exchange_scatter(
        lax.dot_general(
            tokens, grad_cat, (((0,), (0,)), ((), ())), preferred_element_type=jnp.float32
        ).astype(jnp.bfloat16),
        SEQ,
        seq_radices,
    )
    weight_rows = (weight_rows * (1.0 / math.sqrt(SEG * seq_count))).astype(jnp.bfloat16)
    return (
        attended,
        grad_tokens,
        weight_rows[:, :columns],
        weight_rows[:, columns : 2 * columns],
        weight_rows[:, 2 * columns :],
    )


def solution(mesh):
    split_mesh = Mesh(
        mesh.devices.reshape(mesh.shape["seq"] // 2, 2, mesh.shape["fsdp"]), ("z", "core", "fsdp")
    )
    placed = (
        P(SEQ, None),
        P(SEQ, "fsdp"),
        P(SEQ, "fsdp"),
        P(SEQ, "fsdp"),
        P("fsdp"),
        P(SEQ, None, None),
        P(SEQ, "fsdp"),
    )
    return jax.shard_map(
        shards,
        mesh=split_mesh,
        in_specs=placed,
        out_specs=(
            P(SEQ, "fsdp"),
            P(SEQ, "fsdp"),
            P(SEQ, "fsdp"),
            P(SEQ, "fsdp"),
            P(SEQ, "fsdp"),
        ),
        check_vma=False,
    )
```

```python
import math

import jax
import jax.numpy as jnp
from jax import lax
from jax.sharding import Mesh, PartitionSpec as P

HDIM = 128
BLOCK = 128
SEG = 384
NB = 3


EPSILON = 1e-06
SEQ = ("z", "core")


def entering(array, backward):
    count = lax.axis_size("z")
    core = lax.axis_index("core")
    partner = lax.ppermute(array, "core", [(0, 1), (1, 0)])
    pair_total = array + partner
    total = pair_total
    step = 1
    while step < count:
        parts = [total]
        for times in (1, 2, 3):
            shift = step * times
            if shift >= count:
                break
            if backward:
                pairs = [(i, i - shift) for i in range(shift, count)]
            else:
                pairs = [(i, i + shift) for i in range(count - shift)]
            parts.append(lax.ppermute(total, "z", pairs))
        total = sum(parts[1:], parts[0])
        step *= 4
    inside = jnp.where(core == (0 if backward else 1), partner, jnp.zeros_like(partner))
    return (total - pair_total) + inside


def doubling_gather(block, axis, count):
    place = lax.axis_index(axis)
    current = block[None]
    bit = count.bit_length() - 2
    while bit >= 0:
        pairs = [(i, i ^ (1 << bit)) for i in range(count)]
        received = lax.ppermute(current, axis, pairs)
        upper = ((place >> bit) & 1) == 1
        low = jnp.where(upper, received, current)
        high = jnp.where(upper, current, received)
        current = jnp.stack([low, high], axis=1).reshape((-1,) + block.shape)
        bit -= 1
    return current


def radices_for(count):
    radices = []
    while count % 4 == 0:
        radices.append(4)
        count //= 4
    if count > 1:
        radices.append(count)
    return tuple(radices)


def digit_pairs(count, stride, radix, offset):
    pairs = []
    for i in range(count):
        digit = (i // stride) % radix
        pairs.append((i, i + ((digit + offset) % radix - digit) * stride))
    return pairs


def exchange_gather(block, axis, radices):
    count = math.prod(radices)
    place = lax.axis_index(axis)
    strides = [math.prod(radices[:k]) for k in range(len(radices))]
    current = block[None]
    for radix, stride in reversed(list(zip(radices, strides))):
        digit = (place // stride) % radix
        got = [current]
        for offset in range(1, radix):
            got.append(lax.ppermute(current, axis, digit_pairs(count, stride, radix, offset)))
        blocks = []
        for value in range(radix):
            pick = got[0]
            for offset in range(1, radix):
                pick = jnp.where((digit - value) % radix == offset, got[offset], pick)
            blocks.append(pick)
        current = jnp.stack(blocks, axis=1).reshape((-1,) + block.shape)
    return current


def digit_major(array, radices, order):
    rows = array.shape[-1] // math.prod(radices)
    spread = array.reshape(array.shape[:-1] + tuple(reversed(radices)) + (rows,))
    lead = array.ndim - 1
    axes = list(range(lead)) + [lead + len(radices) - 1 - d for d in order] + [lead + len(radices)]
    return spread.transpose(axes).reshape(array.shape)


def exchange_scatter(term, axis, radices, order):
    count = math.prod(radices)
    place = lax.axis_index(axis)
    rows = term.shape[0] // count
    cols = term.shape[1]
    current = term.reshape(count, rows, cols)
    for position in order:
        radix = radices[position]
        stride = math.prod(radices[:position])
        digit = (place // stride) % radix
        split = current.reshape(radix, -1, rows, cols)
        total = lax.dynamic_index_in_dim(split, digit, 0, False).astype(jnp.float32)
        for offset in range(1, radix):
            away = lax.dynamic_index_in_dim(split, (digit + offset) % radix, 0, False)
            moved = lax.ppermute(
                away.astype(jnp.bfloat16), axis, digit_pairs(count, stride, radix, offset)
            )
            total = total + moved.astype(jnp.float32)
        current = total
    return current.reshape(rows, cols)


def halving_scatter(term, axis, count):
    place = lax.axis_index(axis)
    rows = term.shape[0] // count
    current = term.astype(jnp.float32).reshape(count, rows, term.shape[1])
    bit = 0
    while (1 << bit) < count:
        mine = (place >> bit) & 1
        split = current.reshape(current.shape[0] // 2, 2, rows, term.shape[1])
        keep = lax.dynamic_index_in_dim(split, mine, 1, False)
        away = lax.dynamic_index_in_dim(split, 1 - mine, 1, False)
        pairs = [(i, i ^ (1 << bit)) for i in range(count)]
        current = keep + lax.ppermute(away.astype(jnp.bfloat16), axis, pairs).astype(jnp.float32)
        bit += 1
    return current.reshape(rows, term.shape[1])


def allowed_pairs(pattern):
    positions = jnp.arange(SEG)
    block_ids = positions // BLOCK
    selector = (block_ids[:, None] == jnp.arange(NB)[None, :]).astype(jnp.float32)
    spread_out = jnp.dot(
        jnp.dot(selector, pattern.astype(jnp.float32), precision=lax.Precision.HIGHEST),
        selector.T,
        precision=lax.Precision.HIGHEST,
    )
    same_block = (block_ids[:, None] == block_ids[None, :]) & (
        positions[None, :] <= positions[:, None]
    )
    earlier_block = (block_ids[None, :] < block_ids[:, None]) & (spread_out > 0.5)
    return same_block | earlier_block


def add_states(first_term, second_term):
    return first_term + second_term


def shards(tokens, w_query, w_key, w_value, norm_gain, block_mask, cotangent):
    columns = w_query.shape[1]
    heads_here = columns // HDIM
    allowed = allowed_pairs(block_mask[0])
    seq_count = lax.axis_size("z") * lax.axis_size("core")
    fsdp_count = lax.axis_size("fsdp")
    seq_radices = (lax.axis_size("core"),) + radices_for(lax.axis_size("z"))
    fsdp_radices = radices_for(fsdp_count)
    weight_cat = exchange_gather(
        jnp.concatenate([w_query, w_key, w_value], axis=1), SEQ, seq_radices
    ).reshape(-1, 3 * columns)
    projected = jnp.dot(tokens, weight_cat, preferred_element_type=jnp.float32)
    projected = projected.astype(jnp.bfloat16)
    queries = projected[:, :columns].reshape(SEG, heads_here, HDIM)
    key_heads = projected[:, columns : 2 * columns].reshape(SEG, heads_here, HDIM)
    value_heads = projected[:, 2 * columns :].reshape(SEG, heads_here, HDIM)
    increment = jnp.einsum(
        "thd,the->hde", key_heads, value_heads, preferred_element_type=jnp.float32
    )
    state = entering(increment, False)
    state_low = state.astype(jnp.bfloat16)
    scores = jnp.einsum("shd,thd->hst", queries, key_heads, preferred_element_type=jnp.float32)
    weights = jnp.where(allowed[None], scores, 0.0).astype(jnp.bfloat16)
    mixed = jnp.einsum("shd,hde->she", queries, state_low, preferred_element_type=jnp.float32)
    mixed = mixed + jnp.einsum(
        "hst,the->she", weights, value_heads, preferred_element_type=jnp.float32
    )
    scale = lax.rsqrt(jnp.mean(mixed * mixed, axis=-1, keepdims=True) + EPSILON)
    normed = mixed * scale
    gain_heads = norm_gain.reshape(heads_here, HDIM)
    attended = (normed * gain_heads).reshape(SEG, columns).astype(jnp.bfloat16)
    given = cotangent.reshape(SEG, heads_here, HDIM).astype(jnp.float32) * gain_heads
    d_mixed = (scale * (given - normed * jnp.mean(given * normed, axis=-1, keepdims=True))).astype(
        jnp.bfloat16
    )
    d_state = jnp.einsum("shd,she->hde", queries, d_mixed, preferred_element_type=jnp.float32)
    later = entering(d_state, True)
    later_low = later.astype(jnp.bfloat16)
    d_scores = jnp.einsum("she,the->hst", d_mixed, value_heads, preferred_element_type=jnp.float32)
    d_weights = jnp.where(allowed[None], d_scores, 0.0).astype(jnp.bfloat16)
    d_queries = jnp.einsum("she,hde->shd", d_mixed, state_low, preferred_element_type=jnp.float32)
    d_queries = d_queries + jnp.einsum(
        "hst,thd->shd", d_weights, key_heads, preferred_element_type=jnp.float32
    )
    d_keys = jnp.einsum("hst,shd->thd", d_weights, queries, preferred_element_type=jnp.float32)
    d_keys = d_keys + jnp.einsum(
        "the,hde->thd", value_heads, later_low, preferred_element_type=jnp.float32
    )
    d_values = jnp.einsum("hst,she->the", weights, d_mixed, preferred_element_type=jnp.float32)
    d_values = d_values + jnp.einsum(
        "thd,hde->the", key_heads, later_low, preferred_element_type=jnp.float32
    )
    grad_cat = jnp.concatenate(
        [part.reshape(SEG, columns).astype(jnp.bfloat16) for part in (d_queries, d_keys, d_values)],
        axis=1,
    )
    input_rows = exchange_scatter(
        lax.dot_general(
            weight_cat, grad_cat, (((1,), (1,)), ((), ())), preferred_element_type=jnp.float32
        ).astype(jnp.bfloat16),
        "fsdp",
        fsdp_radices,
        tuple(reversed(range(len(fsdp_radices)))),
    )
    grad_tokens = input_rows.T.astype(jnp.bfloat16)
    seq_order = tuple(range(len(seq_radices)))
    weight_rows = exchange_scatter(
        lax.dot_general(
            digit_major(tokens, seq_radices, seq_order),
            grad_cat,
            (((0,), (0,)), ((), ())),
            preferred_element_type=jnp.float32,
        ).astype(jnp.bfloat16),
        SEQ,
        seq_radices,
        seq_order,
    )
    weight_rows = (weight_rows * (1.0 / math.sqrt(SEG * seq_count))).astype(jnp.bfloat16)
    return (
        attended,
        grad_tokens,
        weight_rows[:, :columns],
        weight_rows[:, columns : 2 * columns],
        weight_rows[:, 2 * columns :],
    )


def solution(mesh):
    split_mesh = Mesh(
        mesh.devices.reshape(mesh.shape["seq"] // 2, 2, mesh.shape["fsdp"]), ("z", "core", "fsdp")
    )
    placed = (
        P(SEQ, None),
        P(SEQ, "fsdp"),
        P(SEQ, "fsdp"),
        P(SEQ, "fsdp"),
        P("fsdp"),
        P(SEQ, None, None),
        P(SEQ, "fsdp"),
    )
    return jax.shard_map(
        shards,
        mesh=split_mesh,
        in_specs=placed,
        out_specs=(
            P(SEQ, "fsdp"),
            P(SEQ, "fsdp"),
            P(SEQ, "fsdp"),
            P(SEQ, "fsdp"),
            P(SEQ, "fsdp"),
        ),
        check_vma=False,
    )
```

```python
import math

import jax
import jax.numpy as jnp
from jax import lax
from jax.sharding import Mesh, PartitionSpec as P

HDIM = 128
BLOCK = 128
SEG = 384
NB = 3


EPSILON = 1e-06
SEQ = ("z", "core")


def entering(array, backward):
    count = lax.axis_size("z")
    core = lax.axis_index("core")
    partner = lax.ppermute(array, "core", [(0, 1), (1, 0)])
    pair_total = array + partner
    total = pair_total
    step = 1
    while step < count:
        parts = [total]
        for times in (1, 2, 3):
            shift = step * times
            if shift >= count:
                break
            if backward:
                pairs = [(i, i - shift) for i in range(shift, count)]
            else:
                pairs = [(i, i + shift) for i in range(count - shift)]
            parts.append(lax.ppermute(total, "z", pairs))
        total = sum(parts[1:], parts[0])
        step *= 4
    inside = jnp.where(core == (0 if backward else 1), partner, jnp.zeros_like(partner))
    return (total - pair_total) + inside


def doubling_gather(block, axis, count):
    place = lax.axis_index(axis)
    current = block[None]
    bit = count.bit_length() - 2
    while bit >= 0:
        pairs = [(i, i ^ (1 << bit)) for i in range(count)]
        received = lax.ppermute(current, axis, pairs)
        upper = ((place >> bit) & 1) == 1
        low = jnp.where(upper, received, current)
        high = jnp.where(upper, current, received)
        current = jnp.stack([low, high], axis=1).reshape((-1,) + block.shape)
        bit -= 1
    return current


def radices_for(count):
    radices = []
    while count % 4 == 0:
        radices.append(4)
        count //= 4
    if count > 1:
        radices.append(count)
    return tuple(radices)


def digit_pairs(count, stride, radix, offset):
    pairs = []
    for i in range(count):
        digit = (i // stride) % radix
        pairs.append((i, i + ((digit + offset) % radix - digit) * stride))
    return pairs


def exchange_gather(block, axis, radices):
    count = math.prod(radices)
    place = lax.axis_index(axis)
    strides = [math.prod(radices[:k]) for k in range(len(radices))]
    current = block[None]
    for radix, stride in reversed(list(zip(radices, strides))):
        digit = (place // stride) % radix
        got = [current]
        for offset in range(1, radix):
            got.append(lax.ppermute(current, axis, digit_pairs(count, stride, radix, offset)))
        blocks = []
        for value in range(radix):
            pick = got[0]
            for offset in range(1, radix):
                pick = jnp.where((digit - value) % radix == offset, got[offset], pick)
            blocks.append(pick)
        current = jnp.stack(blocks, axis=1).reshape((-1,) + block.shape)
    return current


def digit_major(array, radices, order):
    rows = array.shape[-1] // math.prod(radices)
    spread = array.reshape(array.shape[:-1] + tuple(reversed(radices)) + (rows,))
    lead = array.ndim - 1
    axes = list(range(lead)) + [lead + len(radices) - 1 - d for d in order] + [lead + len(radices)]
    return spread.transpose(axes).reshape(array.shape)


def exchange_scatter(term, axis, radices, order):
    count = math.prod(radices)
    place = lax.axis_index(axis)
    rows = term.shape[0] // count
    cols = term.shape[1]
    current = term.reshape(count, rows, cols)
    for position in order:
        radix = radices[position]
        stride = math.prod(radices[:position])
        digit = (place // stride) % radix
        split = current.reshape(radix, -1, rows, cols)
        total = lax.dynamic_index_in_dim(split, digit, 0, False).astype(jnp.float32)
        for offset in range(1, radix):
            away = lax.dynamic_index_in_dim(split, (digit + offset) % radix, 0, False)
            moved = lax.ppermute(
                away.astype(jnp.bfloat16), axis, digit_pairs(count, stride, radix, offset)
            )
            total = total + moved.astype(jnp.float32)
        current = total
    return current.reshape(rows, cols)


def exchange_scatter_columns(term, axis, radices, order):
    count = math.prod(radices)
    place = lax.axis_index(axis)
    rows = term.shape[0]
    cols = term.shape[1] // math.prod(radices[position] for position in order)
    current = term
    for position in order:
        radix = radices[position]
        stride = math.prod(radices[:position])
        digit = (place // stride) % radix
        split = current.reshape(rows, radix, -1)
        total = lax.dynamic_index_in_dim(split, digit, 1, False).astype(jnp.float32)
        for offset in range(1, radix):
            away = lax.dynamic_index_in_dim(split, (digit + offset) % radix, 1, False)
            moved = lax.ppermute(
                away.astype(jnp.bfloat16), axis, digit_pairs(count, stride, radix, offset)
            )
            total = total + moved.astype(jnp.float32)
        current = total
    return current.reshape(rows, cols)


def exchange_scatter_grouped(groups, axis, radices, order):
    count = math.prod(radices)
    place = lax.axis_index(axis)
    radix = radices[order[0]]
    stride = math.prod(radices[: order[0]])
    digit = (place // stride) % radix
    total = lax.dynamic_index_in_dim(groups, digit, 0, False).astype(jnp.float32)
    for offset in range(1, radix):
        away = lax.dynamic_index_in_dim(groups, (digit + offset) % radix, 0, False)
        moved = lax.ppermute(
            away.astype(jnp.bfloat16), axis, digit_pairs(count, stride, radix, offset)
        )
        total = total + moved.astype(jnp.float32)
    return exchange_scatter_columns(total, axis, radices, order[1:])


def halving_scatter(term, axis, count):
    place = lax.axis_index(axis)
    rows = term.shape[0] // count
    current = term.astype(jnp.float32).reshape(count, rows, term.shape[1])
    bit = 0
    while (1 << bit) < count:
        mine = (place >> bit) & 1
        split = current.reshape(current.shape[0] // 2, 2, rows, term.shape[1])
        keep = lax.dynamic_index_in_dim(split, mine, 1, False)
        away = lax.dynamic_index_in_dim(split, 1 - mine, 1, False)
        pairs = [(i, i ^ (1 << bit)) for i in range(count)]
        current = keep + lax.ppermute(away.astype(jnp.bfloat16), axis, pairs).astype(jnp.float32)
        bit += 1
    return current.reshape(rows, term.shape[1])


def allowed_pairs(pattern):
    positions = jnp.arange(SEG)
    block_ids = positions // BLOCK
    selector = (block_ids[:, None] == jnp.arange(NB)[None, :]).astype(jnp.float32)
    spread_out = jnp.dot(
        jnp.dot(selector, pattern.astype(jnp.float32), precision=lax.Precision.HIGHEST),
        selector.T,
        precision=lax.Precision.HIGHEST,
    )
    same_block = (block_ids[:, None] == block_ids[None, :]) & (
        positions[None, :] <= positions[:, None]
    )
    earlier_block = (block_ids[None, :] < block_ids[:, None]) & (spread_out > 0.5)
    return same_block | earlier_block


def add_states(first_term, second_term):
    return first_term + second_term


def shards(tokens, w_query, w_key, w_value, norm_gain, block_mask, cotangent):
    columns = w_query.shape[1]
    heads_here = columns // HDIM
    allowed = allowed_pairs(block_mask[0])
    seq_count = lax.axis_size("z") * lax.axis_size("core")
    fsdp_count = lax.axis_size("fsdp")
    seq_radices = (lax.axis_size("core"),) + radices_for(lax.axis_size("z"))
    fsdp_radices = radices_for(fsdp_count)
    weight_cat = exchange_gather(
        jnp.concatenate([w_query, w_key, w_value], axis=1), SEQ, seq_radices
    ).reshape(-1, 3 * columns)
    projected = jnp.dot(tokens, weight_cat, preferred_element_type=jnp.float32)
    projected = projected.astype(jnp.bfloat16)
    queries = projected[:, :columns].reshape(SEG, heads_here, HDIM)
    key_heads = projected[:, columns : 2 * columns].reshape(SEG, heads_here, HDIM)
    value_heads = projected[:, 2 * columns :].reshape(SEG, heads_here, HDIM)
    increment = jnp.einsum(
        "thd,the->hde", key_heads, value_heads, preferred_element_type=jnp.float32
    )
    state = entering(increment, False)
    state_low = state.astype(jnp.bfloat16)
    scores = jnp.einsum("shd,thd->hst", queries, key_heads, preferred_element_type=jnp.float32)
    weights = jnp.where(allowed[None], scores, 0.0).astype(jnp.bfloat16)
    mixed = jnp.einsum("shd,hde->she", queries, state_low, preferred_element_type=jnp.float32)
    mixed = mixed + jnp.einsum(
        "hst,the->she", weights, value_heads, preferred_element_type=jnp.float32
    )
    scale = lax.rsqrt(jnp.mean(mixed * mixed, axis=-1, keepdims=True) + EPSILON)
    normed = mixed * scale
    gain_heads = norm_gain.reshape(heads_here, HDIM)
    attended = (normed * gain_heads).reshape(SEG, columns).astype(jnp.bfloat16)
    given = cotangent.reshape(SEG, heads_here, HDIM).astype(jnp.float32) * gain_heads
    d_mixed = (scale * (given - normed * jnp.mean(given * normed, axis=-1, keepdims=True))).astype(
        jnp.bfloat16
    )
    d_state = jnp.einsum("shd,she->hde", queries, d_mixed, preferred_element_type=jnp.float32)
    later = entering(d_state, True)
    later_low = later.astype(jnp.bfloat16)
    d_scores = jnp.einsum("she,the->hst", d_mixed, value_heads, preferred_element_type=jnp.float32)
    d_weights = jnp.where(allowed[None], d_scores, 0.0).astype(jnp.bfloat16)
    d_queries = jnp.einsum("she,hde->shd", d_mixed, state_low, preferred_element_type=jnp.float32)
    d_queries = d_queries + jnp.einsum(
        "hst,thd->shd", d_weights, key_heads, preferred_element_type=jnp.float32
    )
    d_keys = jnp.einsum("hst,shd->thd", d_weights, queries, preferred_element_type=jnp.float32)
    d_keys = d_keys + jnp.einsum(
        "the,hde->thd", value_heads, later_low, preferred_element_type=jnp.float32
    )
    d_values = jnp.einsum("hst,she->the", weights, d_mixed, preferred_element_type=jnp.float32)
    d_values = d_values + jnp.einsum(
        "thd,hde->the", key_heads, later_low, preferred_element_type=jnp.float32
    )
    grad_cat = jnp.concatenate(
        [part.reshape(SEG, columns).astype(jnp.bfloat16) for part in (d_queries, d_keys, d_values)],
        axis=1,
    )
    fsdp_order = tuple(reversed(range(len(fsdp_radices))))
    grouped_weights = weight_cat.reshape(fsdp_radices[fsdp_order[0]], -1, weight_cat.shape[1])
    input_rows = exchange_scatter_grouped(
        jnp.einsum(
            "tk,gdk->gtd", grad_cat, grouped_weights, preferred_element_type=jnp.float32
        ).astype(jnp.bfloat16),
        "fsdp",
        fsdp_radices,
        fsdp_order,
    )
    grad_tokens = input_rows.astype(jnp.bfloat16)
    seq_order = tuple(range(len(seq_radices)))
    weight_rows = exchange_scatter(
        lax.dot_general(
            digit_major(tokens, seq_radices, seq_order),
            grad_cat,
            (((0,), (0,)), ((), ())),
            preferred_element_type=jnp.float32,
        ).astype(jnp.bfloat16),
        SEQ,
        seq_radices,
        seq_order,
    )
    weight_rows = (weight_rows * (1.0 / math.sqrt(SEG * seq_count))).astype(jnp.bfloat16)
    return (
        attended,
        grad_tokens,
        weight_rows[:, :columns],
        weight_rows[:, columns : 2 * columns],
        weight_rows[:, 2 * columns :],
    )


def solution(mesh):
    split_mesh = Mesh(
        mesh.devices.reshape(mesh.shape["seq"] // 2, 2, mesh.shape["fsdp"]), ("z", "core", "fsdp")
    )
    placed = (
        P(SEQ, None),
        P(SEQ, "fsdp"),
        P(SEQ, "fsdp"),
        P(SEQ, "fsdp"),
        P("fsdp"),
        P(SEQ, None, None),
        P(SEQ, "fsdp"),
    )
    return jax.shard_map(
        shards,
        mesh=split_mesh,
        in_specs=placed,
        out_specs=(
            P(SEQ, "fsdp"),
            P(SEQ, "fsdp"),
            P(SEQ, "fsdp"),
            P(SEQ, "fsdp"),
            P(SEQ, "fsdp"),
        ),
        check_vma=False,
    )
```

```python
import math

import jax
import jax.numpy as jnp
from jax import lax
from jax.sharding import Mesh, PartitionSpec as P

HDIM = 128
BLOCK = 128
SEG = 384
NB = 3


EPSILON = 1e-06
SEQ = ("z", "core")


def entering(array, backward):
    count = lax.axis_size("z")
    core = lax.axis_index("core")
    partner = lax.ppermute(array, "core", [(0, 1), (1, 0)])
    pair_total = array + partner
    total = pair_total
    step = 1
    while step < count:
        parts = [total]
        for times in range(1, count):
            shift = step * times
            if shift >= count:
                break
            if backward:
                pairs = [(i, i - shift) for i in range(shift, count)]
            else:
                pairs = [(i, i + shift) for i in range(count - shift)]
            parts.append(lax.ppermute(total, "z", pairs))
        total = sum(parts[1:], parts[0])
        step *= count
    inside = jnp.where(core == (0 if backward else 1), partner, jnp.zeros_like(partner))
    return (total - pair_total) + inside


def doubling_gather(block, axis, count):
    place = lax.axis_index(axis)
    current = block[None]
    bit = count.bit_length() - 2
    while bit >= 0:
        pairs = [(i, i ^ (1 << bit)) for i in range(count)]
        received = lax.ppermute(current, axis, pairs)
        upper = ((place >> bit) & 1) == 1
        low = jnp.where(upper, received, current)
        high = jnp.where(upper, current, received)
        current = jnp.stack([low, high], axis=1).reshape((-1,) + block.shape)
        bit -= 1
    return current


def radices_for(count):
    radices = []
    while count % 4 == 0:
        radices.append(4)
        count //= 4
    if count > 1:
        radices.append(count)
    return tuple(radices)


def digit_pairs(count, stride, radix, offset):
    pairs = []
    for i in range(count):
        digit = (i // stride) % radix
        pairs.append((i, i + ((digit + offset) % radix - digit) * stride))
    return pairs


def exchange_gather(block, axis, radices):
    count = math.prod(radices)
    place = lax.axis_index(axis)
    strides = [math.prod(radices[:k]) for k in range(len(radices))]
    current = block[None]
    for radix, stride in reversed(list(zip(radices, strides))):
        digit = (place // stride) % radix
        got = [current]
        for offset in range(1, radix):
            got.append(lax.ppermute(current, axis, digit_pairs(count, stride, radix, offset)))
        blocks = []
        for value in range(radix):
            pick = got[0]
            for offset in range(1, radix):
                pick = jnp.where((digit - value) % radix == offset, got[offset], pick)
            blocks.append(pick)
        current = jnp.stack(blocks, axis=1).reshape((-1,) + block.shape)
    return current


def digit_major(array, radices, order):
    rows = array.shape[-1] // math.prod(radices)
    spread = array.reshape(array.shape[:-1] + tuple(reversed(radices)) + (rows,))
    lead = array.ndim - 1
    axes = list(range(lead)) + [lead + len(radices) - 1 - d for d in order] + [lead + len(radices)]
    return spread.transpose(axes).reshape(array.shape)


def exchange_scatter(term, axis, radices, order):
    count = math.prod(radices)
    place = lax.axis_index(axis)
    rows = term.shape[0] // count
    cols = term.shape[1]
    current = term.reshape(count, rows, cols)
    for position in order:
        radix = radices[position]
        stride = math.prod(radices[:position])
        digit = (place // stride) % radix
        split = current.reshape(radix, -1, rows, cols)
        total = lax.dynamic_index_in_dim(split, digit, 0, False).astype(jnp.float32)
        for offset in range(1, radix):
            away = lax.dynamic_index_in_dim(split, (digit + offset) % radix, 0, False)
            moved = lax.ppermute(
                away.astype(jnp.bfloat16), axis, digit_pairs(count, stride, radix, offset)
            )
            total = total + moved.astype(jnp.float32)
        current = total
    return current.reshape(rows, cols)


def halving_scatter(term, axis, count):
    place = lax.axis_index(axis)
    rows = term.shape[0] // count
    current = term.astype(jnp.float32).reshape(count, rows, term.shape[1])
    bit = 0
    while (1 << bit) < count:
        mine = (place >> bit) & 1
        split = current.reshape(current.shape[0] // 2, 2, rows, term.shape[1])
        keep = lax.dynamic_index_in_dim(split, mine, 1, False)
        away = lax.dynamic_index_in_dim(split, 1 - mine, 1, False)
        pairs = [(i, i ^ (1 << bit)) for i in range(count)]
        current = keep + lax.ppermute(away.astype(jnp.bfloat16), axis, pairs).astype(jnp.float32)
        bit += 1
    return current.reshape(rows, term.shape[1])


def allowed_pairs(pattern):
    positions = jnp.arange(SEG)
    block_ids = positions // BLOCK
    selector = (block_ids[:, None] == jnp.arange(NB)[None, :]).astype(jnp.float32)
    spread_out = jnp.dot(
        jnp.dot(selector, pattern.astype(jnp.float32), precision=lax.Precision.HIGHEST),
        selector.T,
        precision=lax.Precision.HIGHEST,
    )
    same_block = (block_ids[:, None] == block_ids[None, :]) & (
        positions[None, :] <= positions[:, None]
    )
    earlier_block = (block_ids[None, :] < block_ids[:, None]) & (spread_out > 0.5)
    return same_block | earlier_block


def add_states(first_term, second_term):
    return first_term + second_term


def shards(tokens, w_query, w_key, w_value, norm_gain, block_mask, cotangent):
    columns = w_query.shape[1]
    heads_here = columns // HDIM
    allowed = allowed_pairs(block_mask[0])
    seq_count = lax.axis_size("z") * lax.axis_size("core")
    fsdp_count = lax.axis_size("fsdp")
    seq_radices = (lax.axis_size("core"),) + radices_for(lax.axis_size("z"))
    fsdp_radices = radices_for(fsdp_count)
    weight_cat = exchange_gather(
        jnp.concatenate([w_query, w_key, w_value], axis=1), SEQ, seq_radices
    ).reshape(-1, 3 * columns)
    projected = jnp.dot(tokens, weight_cat, preferred_element_type=jnp.float32)
    projected = projected.astype(jnp.bfloat16)
    queries = projected[:, :columns].reshape(SEG, heads_here, HDIM)
    key_heads = projected[:, columns : 2 * columns].reshape(SEG, heads_here, HDIM)
    value_heads = projected[:, 2 * columns :].reshape(SEG, heads_here, HDIM)
    increment = jnp.einsum(
        "thd,the->hde", key_heads, value_heads, preferred_element_type=jnp.float32
    )
    state = entering(increment, False)
    state_low = state.astype(jnp.bfloat16)
    scores = jnp.einsum("shd,thd->hst", queries, key_heads, preferred_element_type=jnp.float32)
    weights = jnp.where(allowed[None], scores, 0.0).astype(jnp.bfloat16)
    mixed = jnp.einsum("shd,hde->she", queries, state_low, preferred_element_type=jnp.float32)
    mixed = mixed + jnp.einsum(
        "hst,the->she", weights, value_heads, preferred_element_type=jnp.float32
    )
    scale = lax.rsqrt(jnp.mean(mixed * mixed, axis=-1, keepdims=True) + EPSILON)
    normed = mixed * scale
    gain_heads = norm_gain.reshape(heads_here, HDIM)
    attended = (normed * gain_heads).reshape(SEG, columns).astype(jnp.bfloat16)
    given = cotangent.reshape(SEG, heads_here, HDIM).astype(jnp.float32) * gain_heads
    d_mixed = (scale * (given - normed * jnp.mean(given * normed, axis=-1, keepdims=True))).astype(
        jnp.bfloat16
    )
    d_state = jnp.einsum("shd,she->hde", queries, d_mixed, preferred_element_type=jnp.float32)
    later = entering(d_state, True)
    later_low = later.astype(jnp.bfloat16)
    d_scores = jnp.einsum("she,the->hst", d_mixed, value_heads, preferred_element_type=jnp.float32)
    d_weights = jnp.where(allowed[None], d_scores, 0.0).astype(jnp.bfloat16)
    d_queries = jnp.einsum("she,hde->shd", d_mixed, state_low, preferred_element_type=jnp.float32)
    d_queries = d_queries + jnp.einsum(
        "hst,thd->shd", d_weights, key_heads, preferred_element_type=jnp.float32
    )
    d_keys = jnp.einsum("hst,shd->thd", d_weights, queries, preferred_element_type=jnp.float32)
    d_keys = d_keys + jnp.einsum(
        "the,hde->thd", value_heads, later_low, preferred_element_type=jnp.float32
    )
    d_values = jnp.einsum("hst,she->the", weights, d_mixed, preferred_element_type=jnp.float32)
    d_values = d_values + jnp.einsum(
        "thd,hde->the", key_heads, later_low, preferred_element_type=jnp.float32
    )
    grad_cat = jnp.concatenate(
        [part.reshape(SEG, columns).astype(jnp.bfloat16) for part in (d_queries, d_keys, d_values)],
        axis=1,
    )
    input_rows = exchange_scatter(
        lax.dot_general(
            weight_cat, grad_cat, (((1,), (1,)), ((), ())), preferred_element_type=jnp.float32
        ).astype(jnp.bfloat16),
        "fsdp",
        fsdp_radices,
        tuple(reversed(range(len(fsdp_radices)))),
    )
    grad_tokens = input_rows.T.astype(jnp.bfloat16)
    seq_order = tuple(range(len(seq_radices)))
    weight_rows = exchange_scatter(
        lax.dot_general(
            digit_major(tokens, seq_radices, seq_order),
            grad_cat,
            (((0,), (0,)), ((), ())),
            preferred_element_type=jnp.float32,
        ).astype(jnp.bfloat16),
        SEQ,
        seq_radices,
        seq_order,
    )
    weight_rows = (weight_rows * (1.0 / math.sqrt(SEG * seq_count))).astype(jnp.bfloat16)
    return (
        attended,
        grad_tokens,
        weight_rows[:, :columns],
        weight_rows[:, columns : 2 * columns],
        weight_rows[:, 2 * columns :],
    )


def solution(mesh):
    split_mesh = Mesh(
        mesh.devices.reshape(mesh.shape["seq"] // 2, 2, mesh.shape["fsdp"]), ("z", "core", "fsdp")
    )
    placed = (
        P(SEQ, None),
        P(SEQ, "fsdp"),
        P(SEQ, "fsdp"),
        P(SEQ, "fsdp"),
        P("fsdp"),
        P(SEQ, None, None),
        P(SEQ, "fsdp"),
    )
    return jax.shard_map(
        shards,
        mesh=split_mesh,
        in_specs=placed,
        out_specs=(
            P(SEQ, "fsdp"),
            P(SEQ, "fsdp"),
            P(SEQ, "fsdp"),
            P(SEQ, "fsdp"),
            P(SEQ, "fsdp"),
        ),
        check_vma=False,
    )
```

```python
import math

import jax
import jax.numpy as jnp
from jax import lax
from jax.sharding import Mesh, PartitionSpec as P

HDIM = 128
BLOCK = 128
SEG = 384
NB = 3


EPSILON = 1e-06
SEQ = ("z", "core")


def entering(array, backward):
    count = lax.axis_size("z")
    core = lax.axis_index("core")
    partner = lax.ppermute(array, "core", [(0, 1), (1, 0)])
    pair_total = array + partner
    total = pair_total
    step = 1
    while step < count:
        parts = [total]
        for times in (1, 2, 3):
            shift = step * times
            if shift >= count:
                break
            if backward:
                pairs = [(i, i - shift) for i in range(shift, count)]
            else:
                pairs = [(i, i + shift) for i in range(count - shift)]
            parts.append(lax.ppermute(total, "z", pairs))
        total = sum(parts[1:], parts[0])
        step *= 4
    inside = jnp.where(core == (0 if backward else 1), partner, jnp.zeros_like(partner))
    return (total - pair_total) + inside


def doubling_gather(block, axis, count):
    place = lax.axis_index(axis)
    current = block[None]
    bit = count.bit_length() - 2
    while bit >= 0:
        pairs = [(i, i ^ (1 << bit)) for i in range(count)]
        received = lax.ppermute(current, axis, pairs)
        upper = ((place >> bit) & 1) == 1
        low = jnp.where(upper, received, current)
        high = jnp.where(upper, current, received)
        current = jnp.stack([low, high], axis=1).reshape((-1,) + block.shape)
        bit -= 1
    return current


def radices_for(count):
    radices = []
    while count % 4 == 0:
        radices.append(4)
        count //= 4
    if count > 1:
        radices.append(count)
    return tuple(radices)


def digit_pairs(count, stride, radix, offset):
    pairs = []
    for i in range(count):
        digit = (i // stride) % radix
        pairs.append((i, i + ((digit + offset) % radix - digit) * stride))
    return pairs


def exchange_gather(block, axis, radices):
    count = math.prod(radices)
    place = lax.axis_index(axis)
    strides = [math.prod(radices[:k]) for k in range(len(radices))]
    current = block[None]
    for radix, stride in reversed(list(zip(radices, strides))):
        digit = (place // stride) % radix
        got = [current]
        for offset in range(1, radix):
            got.append(lax.ppermute(current, axis, digit_pairs(count, stride, radix, offset)))
        blocks = []
        for value in range(radix):
            pick = got[0]
            for offset in range(1, radix):
                pick = jnp.where((digit - value) % radix == offset, got[offset], pick)
            blocks.append(pick)
        current = jnp.stack(blocks, axis=1).reshape((-1,) + block.shape)
    return current


def digit_major(array, radices, order):
    rows = array.shape[-1] // math.prod(radices)
    spread = array.reshape(array.shape[:-1] + tuple(reversed(radices)) + (rows,))
    lead = array.ndim - 1
    axes = list(range(lead)) + [lead + len(radices) - 1 - d for d in order] + [lead + len(radices)]
    return spread.transpose(axes).reshape(array.shape)


def exchange_scatter(term, axis, radices, order):
    count = math.prod(radices)
    place = lax.axis_index(axis)
    rows = term.shape[0] // count
    cols = term.shape[1]
    current = term.reshape(count, rows, cols)
    for position in order:
        radix = radices[position]
        stride = math.prod(radices[:position])
        digit = (place // stride) % radix
        split = current.reshape(radix, -1, rows, cols)
        total = lax.dynamic_index_in_dim(split, digit, 0, False).astype(jnp.float32)
        for offset in range(1, radix):
            away = lax.dynamic_index_in_dim(split, (digit + offset) % radix, 0, False)
            moved = lax.ppermute(
                away.astype(jnp.bfloat16), axis, digit_pairs(count, stride, radix, offset)
            )
            total = total + moved.astype(jnp.float32)
        current = total
    return current.reshape(rows, cols)


def halving_scatter(term, axis, count):
    place = lax.axis_index(axis)
    rows = term.shape[0] // count
    current = term.astype(jnp.float32).reshape(count, rows, term.shape[1])
    bit = 0
    while (1 << bit) < count:
        mine = (place >> bit) & 1
        split = current.reshape(current.shape[0] // 2, 2, rows, term.shape[1])
        keep = lax.dynamic_index_in_dim(split, mine, 1, False)
        away = lax.dynamic_index_in_dim(split, 1 - mine, 1, False)
        pairs = [(i, i ^ (1 << bit)) for i in range(count)]
        current = keep + lax.ppermute(away.astype(jnp.bfloat16), axis, pairs).astype(jnp.float32)
        bit += 1
    return current.reshape(rows, term.shape[1])


def allowed_pairs(pattern):
    positions = jnp.arange(SEG)
    block_ids = positions // BLOCK
    selector = (block_ids[:, None] == jnp.arange(NB)[None, :]).astype(jnp.float32)
    spread_out = jnp.dot(
        jnp.dot(selector, pattern.astype(jnp.float32), precision=lax.Precision.HIGHEST),
        selector.T,
        precision=lax.Precision.HIGHEST,
    )
    same_block = (block_ids[:, None] == block_ids[None, :]) & (
        positions[None, :] <= positions[:, None]
    )
    earlier_block = (block_ids[None, :] < block_ids[:, None]) & (spread_out > 0.5)
    return same_block | earlier_block


def add_states(first_term, second_term):
    return first_term + second_term


def shards(tokens, w_query, w_key, w_value, norm_gain, block_mask, cotangent):
    columns = w_query.shape[1]
    heads_here = columns // HDIM
    allowed = allowed_pairs(block_mask[0])
    seq_count = lax.axis_size("z") * lax.axis_size("core")
    fsdp_count = lax.axis_size("fsdp")
    seq_radices = (lax.axis_size("core"),) + radices_for(lax.axis_size("z"))
    fsdp_radices = radices_for(fsdp_count)
    weight_cat = exchange_gather(
        jnp.concatenate([w_query, w_key, w_value], axis=1), SEQ, seq_radices
    ).reshape(-1, 3 * columns)
    projected = jnp.dot(tokens, weight_cat, preferred_element_type=jnp.float32)
    projected = projected.astype(jnp.bfloat16)
    queries = projected[:, :columns].reshape(SEG, heads_here, HDIM)
    key_heads = projected[:, columns : 2 * columns].reshape(SEG, heads_here, HDIM)
    value_heads = projected[:, 2 * columns :].reshape(SEG, heads_here, HDIM)
    increment = jnp.einsum(
        "thd,the->hde", key_heads, value_heads, preferred_element_type=jnp.float32
    )
    state = entering(increment, False)
    state_low = state.astype(jnp.bfloat16)
    scores = jnp.einsum("shd,thd->hst", queries, key_heads, preferred_element_type=jnp.float32)
    weights = jnp.where(allowed[None], scores, 0.0).astype(jnp.bfloat16)
    mixed = jnp.einsum("shd,hde->she", queries, state_low, preferred_element_type=jnp.float32)
    mixed = mixed + jnp.einsum(
        "hst,the->she", weights, value_heads, preferred_element_type=jnp.float32
    )
    scale = lax.rsqrt(jnp.mean(mixed * mixed, axis=-1, keepdims=True) + EPSILON)
    normed = mixed * scale
    gain_heads = norm_gain.reshape(heads_here, HDIM)
    attended = (normed * gain_heads).reshape(SEG, columns).astype(jnp.bfloat16)
    given = cotangent.reshape(SEG, heads_here, HDIM).astype(jnp.float32) * gain_heads
    d_mixed = (scale * (given - normed * jnp.mean(given * normed, axis=-1, keepdims=True))).astype(
        jnp.bfloat16
    )
    d_state = jnp.einsum("shd,she->hde", queries, d_mixed, preferred_element_type=jnp.float32)
    later = entering(d_state, True)
    later_low = later.astype(jnp.bfloat16)
    d_scores = jnp.einsum("she,the->hst", d_mixed, value_heads, preferred_element_type=jnp.float32)
    d_weights = jnp.where(allowed[None], d_scores, 0.0).astype(jnp.bfloat16)
    d_queries = jnp.einsum("she,hde->shd", d_mixed, state_low, preferred_element_type=jnp.float32)
    d_queries = d_queries + jnp.einsum(
        "hst,thd->shd", d_weights, key_heads, preferred_element_type=jnp.float32
    )
    d_keys = jnp.einsum("hst,shd->thd", d_weights, queries, preferred_element_type=jnp.float32)
    d_keys = d_keys + jnp.einsum(
        "the,hde->thd", value_heads, later_low, preferred_element_type=jnp.float32
    )
    d_values = jnp.einsum("hst,she->the", weights, d_mixed, preferred_element_type=jnp.float32)
    d_values = d_values + jnp.einsum(
        "thd,hde->the", key_heads, later_low, preferred_element_type=jnp.float32
    )
    grad_cat = jnp.concatenate(
        [part.reshape(SEG, columns).astype(jnp.bfloat16) for part in (d_queries, d_keys, d_values)],
        axis=1,
    )
    input_rows = exchange_scatter(
        lax.dot_general(
            weight_cat, grad_cat, (((1,), (1,)), ((), ())), preferred_element_type=jnp.float32
        ).astype(jnp.bfloat16),
        "fsdp",
        fsdp_radices,
        tuple(reversed(range(len(fsdp_radices)))),
    )
    grad_tokens = input_rows.T.astype(jnp.bfloat16)
    scatter_radices = seq_radices[:-1] + (2, seq_radices[-1] // 2)
    seq_order = tuple(range(len(scatter_radices)))
    weight_rows = exchange_scatter(
        lax.dot_general(
            digit_major(tokens, scatter_radices, seq_order),
            grad_cat,
            (((0,), (0,)), ((), ())),
            preferred_element_type=jnp.float32,
        ).astype(jnp.bfloat16),
        SEQ,
        scatter_radices,
        seq_order,
    )
    weight_rows = (weight_rows * (1.0 / math.sqrt(SEG * seq_count))).astype(jnp.bfloat16)
    return (
        attended,
        grad_tokens,
        weight_rows[:, :columns],
        weight_rows[:, columns : 2 * columns],
        weight_rows[:, 2 * columns :],
    )


def solution(mesh):
    split_mesh = Mesh(
        mesh.devices.reshape(mesh.shape["seq"] // 2, 2, mesh.shape["fsdp"]), ("z", "core", "fsdp")
    )
    placed = (
        P(SEQ, None),
        P(SEQ, "fsdp"),
        P(SEQ, "fsdp"),
        P(SEQ, "fsdp"),
        P("fsdp"),
        P(SEQ, None, None),
        P(SEQ, "fsdp"),
    )
    return jax.shard_map(
        shards,
        mesh=split_mesh,
        in_specs=placed,
        out_specs=(
            P(SEQ, "fsdp"),
            P(SEQ, "fsdp"),
            P(SEQ, "fsdp"),
            P(SEQ, "fsdp"),
            P(SEQ, "fsdp"),
        ),
        check_vma=False,
    )
```

```python
import math

import jax
import jax.numpy as jnp
from jax import lax
from jax.sharding import Mesh, PartitionSpec as P

HDIM = 128
BLOCK = 128
SEG = 384
NB = 3


EPSILON = 1e-06
SEQ = ("z", "core")


def entering(array, backward):
    count = lax.axis_size("z")
    core = lax.axis_index("core")
    partner = lax.ppermute(array, "core", [(0, 1), (1, 0)])
    pair_total = array + partner
    total = pair_total
    step = 1
    while step < count:
        parts = [total]
        for times in (1, 2, 3):
            shift = step * times
            if shift >= count:
                break
            if backward:
                pairs = [(i, i - shift) for i in range(shift, count)]
            else:
                pairs = [(i, i + shift) for i in range(count - shift)]
            parts.append(lax.ppermute(total, "z", pairs))
        total = sum(parts[1:], parts[0])
        step *= 4
    inside = jnp.where(core == (0 if backward else 1), partner, jnp.zeros_like(partner))
    return (total - pair_total) + inside


def doubling_gather(block, axis, count):
    place = lax.axis_index(axis)
    current = block[None]
    bit = count.bit_length() - 2
    while bit >= 0:
        pairs = [(i, i ^ (1 << bit)) for i in range(count)]
        received = lax.ppermute(current, axis, pairs)
        upper = ((place >> bit) & 1) == 1
        low = jnp.where(upper, received, current)
        high = jnp.where(upper, current, received)
        current = jnp.stack([low, high], axis=1).reshape((-1,) + block.shape)
        bit -= 1
    return current


def radices_for(count):
    radices = []
    while count % 4 == 0:
        radices.append(4)
        count //= 4
    if count > 1:
        radices.append(count)
    return tuple(radices)


def digit_pairs(count, stride, radix, offset):
    pairs = []
    for i in range(count):
        digit = (i // stride) % radix
        pairs.append((i, i + ((digit + offset) % radix - digit) * stride))
    return pairs


def exchange_gather(block, axis, radices):
    count = math.prod(radices)
    place = lax.axis_index(axis)
    strides = [math.prod(radices[:k]) for k in range(len(radices))]
    current = block[None]
    for radix, stride in reversed(list(zip(radices, strides))):
        digit = (place // stride) % radix
        got = [current]
        for offset in range(1, radix):
            got.append(lax.ppermute(current, axis, digit_pairs(count, stride, radix, offset)))
        turned = jnp.stack([got[0]] + got[:0:-1], axis=1)
        doubled = jnp.concatenate([turned, turned], axis=1)
        rolled = lax.dynamic_slice_in_dim(doubled, (radix - digit) % radix, radix, 1)
        current = rolled.reshape((-1,) + block.shape)
    return current


def digit_major(array, radices, order):
    rows = array.shape[-1] // math.prod(radices)
    spread = array.reshape(array.shape[:-1] + tuple(reversed(radices)) + (rows,))
    lead = array.ndim - 1
    axes = list(range(lead)) + [lead + len(radices) - 1 - d for d in order] + [lead + len(radices)]
    return spread.transpose(axes).reshape(array.shape)


def exchange_scatter(term, axis, radices, order):
    count = math.prod(radices)
    place = lax.axis_index(axis)
    rows = term.shape[0] // count
    cols = term.shape[1]
    current = term.reshape(count, rows, cols)
    for position in order:
        radix = radices[position]
        stride = math.prod(radices[:position])
        digit = (place // stride) % radix
        split = current.reshape(radix, -1, rows, cols)
        total = lax.dynamic_index_in_dim(split, digit, 0, False).astype(jnp.float32)
        for offset in range(1, radix):
            away = lax.dynamic_index_in_dim(split, (digit + offset) % radix, 0, False)
            moved = lax.ppermute(
                away.astype(jnp.bfloat16), axis, digit_pairs(count, stride, radix, offset)
            )
            total = total + moved.astype(jnp.float32)
        current = total
    return current.reshape(rows, cols)


def halving_scatter(term, axis, count):
    place = lax.axis_index(axis)
    rows = term.shape[0] // count
    current = term.astype(jnp.float32).reshape(count, rows, term.shape[1])
    bit = 0
    while (1 << bit) < count:
        mine = (place >> bit) & 1
        split = current.reshape(current.shape[0] // 2, 2, rows, term.shape[1])
        keep = lax.dynamic_index_in_dim(split, mine, 1, False)
        away = lax.dynamic_index_in_dim(split, 1 - mine, 1, False)
        pairs = [(i, i ^ (1 << bit)) for i in range(count)]
        current = keep + lax.ppermute(away.astype(jnp.bfloat16), axis, pairs).astype(jnp.float32)
        bit += 1
    return current.reshape(rows, term.shape[1])


def allowed_pairs(pattern):
    positions = jnp.arange(SEG)
    block_ids = positions // BLOCK
    selector = (block_ids[:, None] == jnp.arange(NB)[None, :]).astype(jnp.float32)
    spread_out = jnp.dot(
        jnp.dot(selector, pattern.astype(jnp.float32), precision=lax.Precision.HIGHEST),
        selector.T,
        precision=lax.Precision.HIGHEST,
    )
    same_block = (block_ids[:, None] == block_ids[None, :]) & (
        positions[None, :] <= positions[:, None]
    )
    earlier_block = (block_ids[None, :] < block_ids[:, None]) & (spread_out > 0.5)
    return same_block | earlier_block


def add_states(first_term, second_term):
    return first_term + second_term


def shards(tokens, w_query, w_key, w_value, norm_gain, block_mask, cotangent):
    columns = w_query.shape[1]
    heads_here = columns // HDIM
    allowed = allowed_pairs(block_mask[0])
    seq_count = lax.axis_size("z") * lax.axis_size("core")
    fsdp_count = lax.axis_size("fsdp")
    seq_radices = (lax.axis_size("core"),) + radices_for(lax.axis_size("z"))
    fsdp_radices = radices_for(fsdp_count)
    weight_cat = exchange_gather(
        jnp.concatenate([w_query, w_key, w_value], axis=1), SEQ, seq_radices
    ).reshape(-1, 3 * columns)
    projected = jnp.dot(tokens, weight_cat, preferred_element_type=jnp.float32)
    projected = projected.astype(jnp.bfloat16)
    queries = projected[:, :columns].reshape(SEG, heads_here, HDIM)
    key_heads = projected[:, columns : 2 * columns].reshape(SEG, heads_here, HDIM)
    value_heads = projected[:, 2 * columns :].reshape(SEG, heads_here, HDIM)
    increment = jnp.einsum(
        "thd,the->hde", key_heads, value_heads, preferred_element_type=jnp.float32
    )
    state = entering(increment, False)
    state_low = state.astype(jnp.bfloat16)
    scores = jnp.einsum("shd,thd->hst", queries, key_heads, preferred_element_type=jnp.float32)
    weights = jnp.where(allowed[None], scores, 0.0).astype(jnp.bfloat16)
    mixed = jnp.einsum("shd,hde->she", queries, state_low, preferred_element_type=jnp.float32)
    mixed = mixed + jnp.einsum(
        "hst,the->she", weights, value_heads, preferred_element_type=jnp.float32
    )
    scale = lax.rsqrt(jnp.mean(mixed * mixed, axis=-1, keepdims=True) + EPSILON)
    normed = mixed * scale
    gain_heads = norm_gain.reshape(heads_here, HDIM)
    attended = (normed * gain_heads).reshape(SEG, columns).astype(jnp.bfloat16)
    given = cotangent.reshape(SEG, heads_here, HDIM).astype(jnp.float32) * gain_heads
    d_mixed = (scale * (given - normed * jnp.mean(given * normed, axis=-1, keepdims=True))).astype(
        jnp.bfloat16
    )
    d_state = jnp.einsum("shd,she->hde", queries, d_mixed, preferred_element_type=jnp.float32)
    later = entering(d_state, True)
    later_low = later.astype(jnp.bfloat16)
    d_scores = jnp.einsum("she,the->hst", d_mixed, value_heads, preferred_element_type=jnp.float32)
    d_weights = jnp.where(allowed[None], d_scores, 0.0).astype(jnp.bfloat16)
    d_queries = jnp.einsum("she,hde->shd", d_mixed, state_low, preferred_element_type=jnp.float32)
    d_queries = d_queries + jnp.einsum(
        "hst,thd->shd", d_weights, key_heads, preferred_element_type=jnp.float32
    )
    d_keys = jnp.einsum("hst,shd->thd", d_weights, queries, preferred_element_type=jnp.float32)
    d_keys = d_keys + jnp.einsum(
        "the,hde->thd", value_heads, later_low, preferred_element_type=jnp.float32
    )
    d_values = jnp.einsum("hst,she->the", weights, d_mixed, preferred_element_type=jnp.float32)
    d_values = d_values + jnp.einsum(
        "thd,hde->the", key_heads, later_low, preferred_element_type=jnp.float32
    )
    grad_cat = jnp.concatenate(
        [part.reshape(SEG, columns).astype(jnp.bfloat16) for part in (d_queries, d_keys, d_values)],
        axis=1,
    )
    input_rows = exchange_scatter(
        lax.dot_general(
            weight_cat, grad_cat, (((1,), (1,)), ((), ())), preferred_element_type=jnp.float32
        ).astype(jnp.bfloat16),
        "fsdp",
        fsdp_radices,
        tuple(reversed(range(len(fsdp_radices)))),
    )
    grad_tokens = input_rows.T.astype(jnp.bfloat16)
    seq_order = tuple(range(len(seq_radices)))
    weight_rows = exchange_scatter(
        lax.dot_general(
            digit_major(tokens, seq_radices, seq_order),
            grad_cat,
            (((0,), (0,)), ((), ())),
            preferred_element_type=jnp.float32,
        ).astype(jnp.bfloat16),
        SEQ,
        seq_radices,
        seq_order,
    )
    weight_rows = (weight_rows * (1.0 / math.sqrt(SEG * seq_count))).astype(jnp.bfloat16)
    return (
        attended,
        grad_tokens,
        weight_rows[:, :columns],
        weight_rows[:, columns : 2 * columns],
        weight_rows[:, 2 * columns :],
    )


def solution(mesh):
    split_mesh = Mesh(
        mesh.devices.reshape(mesh.shape["seq"] // 2, 2, mesh.shape["fsdp"]), ("z", "core", "fsdp")
    )
    placed = (
        P(SEQ, None),
        P(SEQ, "fsdp"),
        P(SEQ, "fsdp"),
        P(SEQ, "fsdp"),
        P("fsdp"),
        P(SEQ, None, None),
        P(SEQ, "fsdp"),
    )
    return jax.shard_map(
        shards,
        mesh=split_mesh,
        in_specs=placed,
        out_specs=(
            P(SEQ, "fsdp"),
            P(SEQ, "fsdp"),
            P(SEQ, "fsdp"),
            P(SEQ, "fsdp"),
            P(SEQ, "fsdp"),
        ),
        check_vma=False,
    )
```
